256 devices in a mesh: member: 128 (over z, x, y), segment: 2 (over core).
Axes of the slice: x: 4, y: 4, z: 8, core: 2. Of those that a mesh axis runs over, the one named last changes fastest.
Arguments:
- start_noise: float32 [128, 4, 4, 256], P('member'), may hold values from -6 to 6
- reg_means: float32 [128, 4, 32, 4, 256], P('member'), may hold values from -6 to 6
- hour_owner: int32 [4], replicated, may hold values from 0 to 127
- member_tile: int32 [128], P('member'), may hold values from 0 to 31
- sigmas: float32 [9], replicated, may hold values from 0.3 to 22, as said below
- lift_weight: float32 [8, 128], replicated, may hold values from -2 to 2
- noise_embed: float32 [128], replicated, may hold values from -6 to 6
- section_conv: bfloat16 [2, 9, 128, 128], P('segment'), may hold values from -0.1875 to 0.1875
- section_gain: bfloat16 [2, 128], P('segment'), may hold values from 0.5 to 2
- out_weight: float32 [128, 4], replicated, may hold values from -0.5 to 0.5
Outputs:
- downscaled: float32 [4, 128, 4, 256], P('segment', 'member')
The draws below stay inside these ranges and needn't reach their ends.
Inputs may be any that keep to these rules, and one draw needn't show every extreme that they name: `sigmas`: strictly decreasing and positive.
All inputs are finite; a program needn't handle non-finite values.
Results may differ from the reference program's by a relative error of at most 0.00038.
Values may be sent and summed in bfloat16 or wider, within the bound.
No kernel may reach another device: no remote copies, remote signals or barrier semaphores. Data moves between devices by JAX's collectives and lax.ppermute only.
A program may use at most 64 MiB of HBM per device.

```python
import math
import jax
import jax.numpy as jnp
from jax import lax

SIDE = 16
PIX = 256
C = 128
CIN = 4
HOURS = 4
STEPS = 8
TILES = 32
MEMBERS = 128


def draw_sigmas(key, part):
    levels = jnp.arange(STEPS + 1).astype(jnp.float32)
    jitter = jax.random.uniform(key, (STEPS + 1,), jnp.float32, 0.9, 1.1)
    return (20.0 * jnp.power(jnp.float32(0.6), levels) * jitter).astype(jnp.float32)


def set_ends(entries, own_key, low, high):
    extent = entries.shape
    index_at = [jax.random.randint(jax.random.fold_in(own_key, axis), (), 0, extent[axis]) for axis in range(len(extent))]
    entries = entries.at[tuple(index_at)].set(low)
    longest = extent.index(max(extent))
    index_at[longest] = (index_at[longest] + 1) % extent[longest]
    return entries.at[tuple(index_at)].set(high)


def block_levels(key, shape, split, low, top_value):
    level = 1.0
    for dim, shards_of in split:
        heights = jax.random.uniform(jax.random.fold_in(jax.random.fold_in(key, 6), dim), (shards_of,), jnp.float32, low / len(split), top_value / len(split))
        level = level * jnp.repeat(jnp.exp(heights), shape[dim] // shards_of).reshape((-1,) + (1,) * (len(shape) - 1 - dim))
    return level


def centred(rng, dims, scale, reach, split=(), held_as=jnp.bfloat16):
    array = scale * jax.random.normal(rng, dims, jnp.float32)
    if split:
        array = array * block_levels(rng, dims, split, -0.22, 0.18)
    return jnp.clip(array, -reach, reach).astype(held_as)


def setup_inputs(seed: int = 0) -> dict:
    key_of = jax.random.split(jax.random.key(seed), 11)
    start_noise = centred(key_of[0], (MEMBERS, HOURS, CIN, PIX), 1.0, 6.0, ((0, 128),), jnp.float32)
    reg_means = centred(key_of[1], (MEMBERS, HOURS, TILES, CIN, PIX), 1.0, 6.0, ((0, 128),), jnp.float32)
    hour_owner = set_ends(jax.random.randint(key_of[2], (HOURS,), 0, MEMBERS), jax.random.fold_in(key_of[2], 1), 0, MEMBERS - 1).astype(jnp.int32)
    member_tile = set_ends(jax.random.randint(key_of[3], (MEMBERS,), 0, TILES), jax.random.fold_in(key_of[3], 1), 0, TILES - 1).astype(jnp.int32)
    sigmas = draw_sigmas(jax.random.fold_in(key_of[10], 71), 0)
    lift_weight = centred(key_of[5], (2 * CIN, C), (2 * CIN) ** -0.5, 2.0, (), jnp.float32)
    noise_embed = centred(key_of[6], (C,), 1.0, 6.0, (), jnp.float32)
    section_conv = centred(key_of[7], (2, 9, C, C), (9 * C) ** -0.5, 0.1875, ((0, 2),))
    section_gain = jnp.clip(jnp.exp(math.log(2.0) - 1.3862944 * jax.random.uniform(key_of[8], (2, C), jnp.float32) ** block_levels(key_of[8], (2, C), ((0, 2),), -0.2, 0.2)), 0.5, 2.0).astype(jnp.bfloat16)
    out_weight = centred(key_of[9], (C, CIN), C ** -0.5, 0.5, (), jnp.float32)
    return dict(start_noise=start_noise, reg_means=reg_means, hour_owner=hour_owner, member_tile=member_tile, sigmas=sigmas, lift_weight=lift_weight, noise_embed=noise_embed, section_conv=section_conv, section_gain=section_gain, out_weight=out_weight)


EPSILON = 1e-06
DATA_VAR = 0.25

def rms_scale(values):
    return values * lax.rsqrt(lax.optimization_barrier(jnp.mean(values * values, axis=-1, keepdims=True)) + EPSILON)

def conv_three(gated, kernel, tile_side):
    batched = gated.shape[0]
    channels = gated.shape[-1]
    grid_view = gated.reshape(batched, tile_side, tile_side, channels)
    padded = jnp.pad(grid_view, ((0, 0), (1, 1), (1, 1), (0, 0)))
    windows = [padded[:, vertical:vertical + tile_side, lateral:lateral + tile_side, :] for vertical in range(3) for lateral in range(3)]
    stacked = jnp.concatenate(windows, axis=-1).reshape(batched * tile_side * tile_side, 9 * channels)
    summed = jnp.dot(stacked, kernel.reshape(9 * channels, kernel.shape[-1]), preferred_element_type=jnp.float32)
    return summed.reshape(batched, tile_side * tile_side, kernel.shape[-1])

def lift_inputs(state_now, mean_now, sigma_now, lift_weight, noise_embed):
    scale_in = lax.rsqrt(sigma_now * sigma_now + DATA_VAR)
    stacked = jnp.concatenate([state_now * scale_in, mean_now], axis=1)
    lifted = jnp.einsum('bcp,cd->bpd', stacked, lift_weight, precision=lax.Precision.HIGHEST)
    return lifted + jnp.log(sigma_now) / 4.0 * noise_embed

def encode(lifted, kernel, gain, tile_side):
    gated = jax.nn.silu(rms_scale(lifted) * gain.astype(jnp.float32)).astype(jnp.bfloat16)
    return (lifted + conv_three(gated, kernel, tile_side)).astype(jnp.bfloat16)

def decode(encoded, skipped, kernel, gain, out_weight, tile_side):
    widened = encoded.astype(jnp.float32)
    gated = jax.nn.silu(rms_scale(widened) * gain.astype(jnp.float32)).astype(jnp.bfloat16)
    merged = widened + conv_three(gated, kernel, tile_side) + skipped.astype(jnp.float32)
    return jnp.einsum('bpd,dc->bcp', jax.nn.silu(rms_scale(merged)), out_weight, precision=lax.Precision.HIGHEST)

def euler_step(state_now, net_out, sigma_now, sigma_next):
    spread = sigma_now * sigma_now + DATA_VAR
    denoised = DATA_VAR / spread * state_now + 0.5 * sigma_now * lax.rsqrt(spread) * net_out
    return state_now + (sigma_next - sigma_now) / sigma_now * (state_now - denoised)

def reference(start_noise, reg_means, hour_owner, member_tile, sigmas, lift_weight, noise_embed, section_conv, section_gain, out_weight):
    results = []
    for hour_index in range(HOURS):
        chosen = lax.dynamic_index_in_dim(reg_means, hour_owner[hour_index].astype(jnp.int32), 0, keepdims=False)[hour_index]
        mean_field = jnp.take(chosen, member_tile.astype(jnp.int32), axis=0)
        state_now = sigmas[0] * start_noise[:, hour_index]
        for step_index in range(STEPS):
            lifted = lift_inputs(state_now, mean_field, sigmas[step_index], lift_weight, noise_embed)
            encoded = encode(lifted, section_conv[0], section_gain[0], SIDE)
            net_out = decode(encoded, lifted.astype(jnp.bfloat16), section_conv[1], section_gain[1], out_weight, SIDE)
            state_now = euler_step(state_now, net_out, sigmas[step_index], sigmas[step_index + 1])
        results.append(mean_field + state_now)
    return jnp.stack(results)
```

```python
import numpy as np
import jax
import jax.numpy as jnp
from jax import lax
from jax.sharding import PartitionSpec as P

SIDE = 16
HOURS = 4
STEPS = 8


EPSILON = 1e-06
DATA_VAR = 0.25


def ring_routes(mesh):
    devices = np.asarray(mesh.devices)[:, 0]
    coords = [tuple(d.coords[:3]) for d in devices]
    where = {c: i for i, c in enumerate(coords)}
    sizes = [len({c[a] for c in coords}) for a in range(3)]
    routes = []
    for axis in sorted(range(3), key=lambda a: -sizes[a]):
        n = sizes[axis]
        if n == 1:
            continue
        shifts = []
        distance = 1
        while distance < n:
            pairs = {}
            for sign in (1, -1):
                pair = []
                for i, c in enumerate(coords):
                    moved = list(c)
                    moved[axis] = (c[axis] + sign * distance) % n
                    pair.append((i, where[tuple(moved)]))
                pairs[sign] = tuple(pair)
            shifts.append(pairs)
            distance *= 2
        routes.append((n, shifts))
    return routes


def broadcast_sum(block, routes):
    half = block.shape[0] // 2
    up, down = block[:half], block[half:]
    for n, shifts in routes:
        if n & (n - 1):
            raise ValueError("ring size")
        for pairs in shifts:
            up = up + lax.ppermute(up, "member", pairs[1])
            down = down + lax.ppermute(down, "member", pairs[-1])
    return jnp.concatenate([up, down], axis=0)


def rms_scale(values):
    return values * lax.rsqrt(jnp.mean(values * values, axis=-1, keepdims=True) + EPSILON)


def conv_three(gated, kernel, tile_side):
    batched = gated.shape[0]
    channels = gated.shape[-1]
    grid_view = gated.reshape(batched, tile_side, tile_side, channels)
    padded = jnp.pad(grid_view, ((0, 0), (1, 1), (1, 1), (0, 0)))
    windows = [
        padded[:, vertical : vertical + tile_side, lateral : lateral + tile_side, :]
        for vertical in range(3)
        for lateral in range(3)
    ]
    stacked = jnp.concatenate(windows, axis=-1).reshape(
        batched * tile_side * tile_side, 9 * channels
    )
    summed = jnp.dot(
        stacked, kernel.reshape(9 * channels, kernel.shape[-1]), preferred_element_type=jnp.float32
    )
    return summed.reshape(batched, tile_side * tile_side, kernel.shape[-1])


def network(lifted, kernels, gains, out_weight, tile_side):
    gated = jax.nn.silu(rms_scale(lifted) * gains[0].astype(jnp.float32)).astype(jnp.bfloat16)
    encoded = (lifted + conv_three(gated, kernels[0], tile_side)).astype(jnp.bfloat16)
    widened = encoded.astype(jnp.float32)
    gated = jax.nn.silu(rms_scale(widened) * gains[1].astype(jnp.float32)).astype(jnp.bfloat16)
    skipped = lifted.astype(jnp.bfloat16).astype(jnp.float32)
    merged = widened + conv_three(gated, kernels[1], tile_side) + skipped
    return jnp.einsum(
        "bpd,dc->bcp", jax.nn.silu(rms_scale(merged)), out_weight, precision=lax.Precision.HIGHEST
    )


def euler_step(state_now, net_out, sigma_now, sigma_next):
    spread = sigma_now * sigma_now + DATA_VAR
    denoised = DATA_VAR / spread * state_now + 0.5 * sigma_now * lax.rsqrt(spread) * net_out
    return state_now + (sigma_next - sigma_now) / sigma_now * (state_now - denoised)


def make_body(routes):
    def body(
        start_noise,
        reg_means,
        hour_owner,
        member_tile,
        sigmas,
        lift_weight,
        noise_embed,
        section_conv,
        section_gain,
        out_weight,
    ):
        tile_side = SIDE
        segment_index = lax.axis_index("segment")
        is_first = segment_index == 0
        half_hours = HOURS // lax.axis_size("segment")
        first_hour = segment_index * half_hours
        variables = start_noise.shape[2]

        swap = [(0, 1), (1, 0)]
        other_conv = lax.ppermute(section_conv, "segment", swap)
        other_gain = lax.ppermute(section_gain, "segment", swap)
        kernels = (
            jnp.where(is_first, section_conv[0], other_conv[0]),
            jnp.where(is_first, other_conv[0], section_conv[0]),
        )
        gains = (
            jnp.where(is_first, section_gain[0], other_gain[0]),
            jnp.where(is_first, other_gain[0], section_gain[0]),
        )

        owners = lax.dynamic_slice_in_dim(hour_owner, first_hour, half_hours, 0)
        mine = lax.dynamic_slice_in_dim(reg_means[0], first_hour, half_hours, 0)
        is_owner = lax.axis_index("member") == owners
        kept = jnp.where(is_owner[:, None, None, None], mine, 0).astype(mine.dtype)
        arrived = broadcast_sum(kept, routes)
        means = lax.dynamic_index_in_dim(arrived, member_tile[0], 1, keepdims=False)

        noise = lax.dynamic_slice_in_dim(start_noise[0], first_hour, half_hours, 0)
        states = sigmas[0] * noise
        mean_lift = jnp.einsum(
            "bcp,cd->bpd", means, lift_weight[variables:], precision=lax.Precision.HIGHEST
        )
        def one_step(step_index, states):
            sigma_now = lax.dynamic_index_in_dim(sigmas, step_index, 0, keepdims=False)
            sigma_next = lax.dynamic_index_in_dim(sigmas, step_index + 1, 0, keepdims=False)
            scale_in = lax.rsqrt(sigma_now * sigma_now + DATA_VAR)
            lifted = jnp.einsum(
                "bcp,cd->bpd",
                states * scale_in,
                lift_weight[:variables],
                precision=lax.Precision.HIGHEST,
            )
            lifted = lifted + mean_lift + jnp.log(sigma_now) / 4.0 * noise_embed
            net_out = network(lifted, kernels, gains, out_weight, tile_side)
            return euler_step(states, net_out, sigma_now, sigma_next)

        states = lax.fori_loop(0, STEPS, one_step, states)
        return (means + states)[:, None]

    return body


def solution(mesh):
    placed = (
        P("member", None, None, None),
        P("member", None, None, None, None),
        P(),
        P("member"),
        P(),
        P(),
        P(),
        P("segment", None, None, None),
        P("segment", None),
        P(),
    )
    return jax.shard_map(
        make_body(ring_routes(mesh)),
        mesh=mesh,
        in_specs=placed,
        out_specs=P("segment", "member", None, None),
        check_vma=False,
    )
```

```python
import numpy as np
import jax
import jax.numpy as jnp
from jax import lax
from jax.sharding import PartitionSpec as P
from jax.experimental import pallas as pl
from jax.experimental.pallas import tpu as pltpu

SIDE = 16
HOURS = 4
STEPS = 8


EPSILON = 1e-06
DATA_VAR = 0.25


def ring_routes(mesh):
    devices = np.asarray(mesh.devices)[:, 0]
    coords = [tuple(d.coords[:3]) for d in devices]
    where = {c: i for i, c in enumerate(coords)}
    sizes = [len({c[a] for c in coords}) for a in range(3)]

    def shift_pairs(axis, distance):
        n = sizes[axis]
        pairs = []
        for i, c in enumerate(coords):
            moved = list(c)
            moved[axis] = (c[axis] + distance) % n
            pairs.append((i, where[tuple(moved)]))
        return tuple(pairs)

    stages = []
    for axis in sorted(range(3), key=lambda a: sizes[a]):
        n = sizes[axis]
        if n == 1:
            continue
        if n & (n - 1):
            raise ValueError("ring size")
        if n == 2:
            stages.append((shift_pairs(axis, 1),))
            continue
        stages.append(tuple(shift_pairs(axis, d) for d in (1, -1, 2)))
        distance = 4
        while distance < n:
            stages.append((shift_pairs(axis, distance),))
            distance *= 2
    return stages


def broadcast_sum(block, stages):
    for stage in stages:
        arrived = [lax.ppermute(block, "member", pairs) for pairs in stage]
        for part in arrived:
            block = block + part
    return block


def rms_scale(values):
    return values * lax.rsqrt(jnp.mean(values * values, axis=-1, keepdims=True) + EPSILON)


def silu(values):
    return values / (1.0 + jnp.exp(-values))


def chain_kernel(coef_ref, state_ref, means_ref, lift_ref, embed_ref, conv_ref, gain_ref, out_ref, result_ref):
    rows, lanes = state_ref.shape
    pixel = lax.broadcasted_iota(jnp.int32, (rows, lanes), 0) % (SIDE * SIDE)
    row = pixel // SIDE
    col = pixel % SIDE
    offsets = [(a, b) for a in (-1, 0, 1) for b in (-1, 0, 1)]
    valid = [
        (row + a >= 0) & (row + a < SIDE) & (col + b >= 0) & (col + b < SIDE) for a, b in offsets
    ]

    def conv(gated, index):
        windows = []
        for (a, b), keep in zip(offsets, valid):
            distance = a * SIDE + b
            moved = gated if distance == 0 else pltpu.roll(gated, (-distance) % rows, 0)
            windows.append(jnp.where(keep, moved, 0.0).astype(jnp.bfloat16))
        stacked = jnp.concatenate(windows, axis=1)
        return jnp.dot(stacked, conv_ref[index], preferred_element_type=jnp.float32)

    means = means_ref[...]
    embed = embed_ref[...]
    gain_enc = gain_ref[0:1, :]
    gain_dec = gain_ref[1:2, :]

    def one_step(step, state):
        scale_in = coef_ref[step * 5 + 0]
        level = coef_ref[step * 5 + 1]
        keep_state = coef_ref[step * 5 + 2]
        keep_net = coef_ref[step * 5 + 3]
        move = coef_ref[step * 5 + 4]
        inputs = state * scale_in + means
        lifted = jnp.dot(
            inputs, lift_ref[...], precision=lax.Precision.HIGHEST, preferred_element_type=jnp.float32
        )
        lifted = lifted + level * embed
        gated = silu(rms_scale(lifted) * gain_enc)
        encoded = (lifted + conv(gated, 0)).astype(jnp.bfloat16).astype(jnp.float32)
        gated = silu(rms_scale(encoded) * gain_dec)
        skipped = lifted.astype(jnp.bfloat16).astype(jnp.float32)
        merged = encoded + conv(gated, 1) + skipped
        net_out = jnp.dot(
            silu(rms_scale(merged)),
            out_ref[...],
            precision=lax.Precision.HIGHEST,
            preferred_element_type=jnp.float32,
        )
        denoised = keep_state * state + keep_net * net_out
        return state + move * (state - denoised)

    result_ref[...] = lax.fori_loop(0, STEPS, one_step, state_ref[...])


def run_chain(coefs, state, means, lift, embed, kernels, gains, out_weight):
    vmem = pltpu.MemorySpace.VMEM
    return pl.pallas_call(
        chain_kernel,
        out_shape=jax.ShapeDtypeStruct(state.shape, jnp.float32),
        in_specs=[pl.BlockSpec(memory_space=pltpu.MemorySpace.SMEM)]
        + [pl.BlockSpec(memory_space=vmem)] * 7,
        out_specs=pl.BlockSpec(memory_space=vmem),
    )(coefs, state, means, lift, embed, kernels, gains, out_weight)


def step_coefficients(sigmas):
    sigma_now = sigmas[:-1]
    sigma_next = sigmas[1:]
    spread = sigma_now * sigma_now + DATA_VAR
    return jnp.stack(
        [
            lax.rsqrt(spread),
            jnp.log(sigma_now) / 4.0,
            DATA_VAR / spread,
            0.5 * sigma_now * lax.rsqrt(spread),
            (sigma_next - sigma_now) / sigma_now,
        ],
        axis=1,
    ).reshape(-1)


def to_lanes(fields, first_lane, lanes):
    batched, variables, pixels = fields.shape
    flat = jnp.transpose(fields, (0, 2, 1)).reshape(batched * pixels, variables)
    return jnp.pad(flat, ((0, 0), (first_lane, lanes - first_lane - variables)))


def make_body(routes):
    def body(
        start_noise,
        reg_means,
        hour_owner,
        member_tile,
        sigmas,
        lift_weight,
        noise_embed,
        section_conv,
        section_gain,
        out_weight,
    ):
        segment_index = lax.axis_index("segment")
        is_first = segment_index == 0
        half_hours = HOURS // lax.axis_size("segment")
        first_hour = segment_index * half_hours
        variables = start_noise.shape[2]
        pixels = start_noise.shape[3]
        channels = section_conv.shape[-1]

        swap = [(0, 1), (1, 0)]
        other_conv = lax.ppermute(section_conv, "segment", swap)
        other_gain = lax.ppermute(section_gain, "segment", swap)
        kernels = jnp.stack(
            [
                jnp.where(is_first, section_conv[0], other_conv[0]),
                jnp.where(is_first, other_conv[0], section_conv[0]),
            ]
        ).reshape(2, 9 * channels, channels)
        gains = jnp.stack(
            [
                jnp.where(is_first, section_gain[0], other_gain[0]),
                jnp.where(is_first, other_gain[0], section_gain[0]),
            ]
        ).astype(jnp.float32)

        owners = lax.dynamic_slice_in_dim(hour_owner, first_hour, half_hours, 0)
        mine = lax.dynamic_slice_in_dim(reg_means[0], first_hour, half_hours, 0)
        is_owner = lax.axis_index("member") == owners
        kept = jnp.where(is_owner[:, None, None, None], mine, 0).astype(mine.dtype)
        arrived = broadcast_sum(kept, routes)
        means = lax.dynamic_index_in_dim(arrived, member_tile[0], 1, keepdims=False)

        noise = lax.dynamic_slice_in_dim(start_noise[0], first_hour, half_hours, 0)
        states = sigmas[0] * noise
        lift = jnp.pad(lift_weight, ((0, channels - 2 * variables), (0, 0)))
        out_pad = jnp.pad(out_weight, ((0, 0), (0, channels - variables)))
        finished = run_chain(
            step_coefficients(sigmas),
            to_lanes(states, 0, channels),
            to_lanes(means, variables, channels),
            lift,
            noise_embed[None, :],
            kernels,
            gains,
            out_pad,
        )
        finished = finished[:, :variables].reshape(half_hours, pixels, variables)
        return (means + jnp.transpose(finished, (0, 2, 1)))[:, None]

    return body


def solution(mesh):
    placed = (
        P("member", None, None, None),
        P("member", None, None, None, None),
        P(),
        P("member"),
        P(),
        P(),
        P(),
        P("segment", None, None, None),
        P("segment", None),
        P(),
    )
    return jax.shard_map(
        make_body(ring_routes(mesh)),
        mesh=mesh,
        in_specs=placed,
        out_specs=P("segment", "member", None, None),
        check_vma=False,
    )
```

```python
import numpy as np
import jax
import jax.numpy as jnp
from jax import lax
from jax.sharding import PartitionSpec as P
from jax.experimental import pallas as pl
from jax.experimental.pallas import tpu as pltpu

SIDE = 16
HOURS = 4
STEPS = 8


EPSILON = 1e-06
DATA_VAR = 0.25


def ring_routes(mesh):
    devices = np.asarray(mesh.devices)[:, 0]
    coords = [tuple(d.coords[:3]) for d in devices]
    where = {c: i for i, c in enumerate(coords)}
    sizes = [len({c[a] for c in coords}) for a in range(3)]
    axes = [a for a in sorted(range(3), key=lambda a: sizes[a]) if sizes[a] > 1]

    def shift_pairs(axis, distance):
        pairs = []
        for i, c in enumerate(coords):
            moved = list(c)
            moved[axis] = (c[axis] + distance) % sizes[axis]
            pairs.append((i, where[tuple(moved)]))
        return tuple(pairs)

    rings = []
    for axis in axes:
        n = sizes[axis]
        shifts = {d: shift_pairs(axis, d) for d in range(-n + 1, n) if d}
        position = tuple(c[axis] for c in coords)
        rings.append((n, shifts, position))
    return rings


def window_stages(n):
    if n & (n - 1):
        raise ValueError("ring size")
    if n == 2:
        return [(1,)]
    stages = [(1, -1, 2)]
    distance = 4
    while distance < n:
        stages.append((distance,))
        distance *= 2
    return stages


def broadcast_sum(block, rings):
    for n, shifts, _ in rings:
        for stage in window_stages(n):
            arrived = [lax.ppermute(block, "member", shifts[d]) for d in stage]
            for part in arrived:
                block = block + part
    return block


def reversed_pairs(pairs):
    return tuple((j, i) for i, j in pairs)


def targeted_mean(kept, tile, rings):
    (_, shifts_a, _), (_, shifts_b, _), (size_z, shifts_z, position_z) = rings
    member = lax.axis_index("member")
    at_z = jnp.asarray(position_z, jnp.int32)[member]
    slots = jnp.arange(size_z, dtype=jnp.int32)

    tiles_z = jnp.where(slots == at_z, tile, 0)
    for d in range(1, size_z):
        came = lax.ppermute(tile[None], "member", shifts_z[d])
        tiles_z = tiles_z + jnp.where(slots == (at_z - d) % size_z, came[0], 0)
    wanted = {d: lax.ppermute(tiles_z, "member", reversed_pairs(shifts_b[d])) for d in (1, -1, 2)}

    block = kept
    arrived = [lax.ppermute(block, "member", shifts_a[d]) for d in (1, -1, 2)]
    for part in arrived:
        block = block + part

    sent = {d: jnp.take(block, wanted[d], axis=1, mode="clip") for d in (1, -1, 2)}
    arrived = [lax.ppermute(sent[d], "member", shifts_b[d]) for d in (1, -1, 2)]
    block = jnp.take(block, tiles_z, axis=1, mode="clip")
    for part in arrived:
        block = block + part

    def pick(block, first):
        served = jnp.stack([first % size_z, (first + size_z // 2) % size_z])
        return jnp.take(block, served, axis=1, mode="clip")

    arrived = [lax.ppermute(pick(block, at_z + d), "member", shifts_z[d]) for d in (1, -1, 2)]
    block = pick(block, at_z)
    for part in arrived:
        block = block + part

    arrived = lax.ppermute(block[:, 1], "member", shifts_z[size_z // 2])
    return block[:, 0] + arrived


def rms_scale(values):
    return values * lax.rsqrt(jnp.mean(values * values, axis=-1, keepdims=True) + EPSILON)


def silu(values):
    return values / (1.0 + jnp.exp(-values))


def chain_kernel(coef_ref, state_ref, means_ref, lift_ref, embed_ref, conv_ref, gain_ref, out_ref, result_ref):
    rows, lanes = state_ref.shape
    pixel = lax.broadcasted_iota(jnp.int32, (rows, lanes), 0) % (SIDE * SIDE)
    row = pixel // SIDE
    col = pixel % SIDE
    offsets = [(a, b) for a in (-1, 0, 1) for b in (-1, 0, 1)]
    valid = [
        (row + a >= 0) & (row + a < SIDE) & (col + b >= 0) & (col + b < SIDE) for a, b in offsets
    ]

    def conv(gated, index):
        windows = []
        for (a, b), keep in zip(offsets, valid):
            distance = a * SIDE + b
            moved = gated if distance == 0 else pltpu.roll(gated, (-distance) % rows, 0)
            windows.append(jnp.where(keep, moved, 0.0).astype(jnp.bfloat16))
        stacked = jnp.concatenate(windows, axis=1)
        return jnp.dot(stacked, conv_ref[index], preferred_element_type=jnp.float32)

    means = means_ref[...]
    embed = embed_ref[...]
    gain_enc = gain_ref[0:1, :]
    gain_dec = gain_ref[1:2, :]

    def one_step(step, state):
        scale_in = coef_ref[step * 5 + 0]
        level = coef_ref[step * 5 + 1]
        keep_state = coef_ref[step * 5 + 2]
        keep_net = coef_ref[step * 5 + 3]
        move = coef_ref[step * 5 + 4]
        inputs = state * scale_in + means
        lifted = jnp.dot(
            inputs, lift_ref[...], precision=lax.Precision.HIGHEST, preferred_element_type=jnp.float32
        )
        lifted = lifted + level * embed
        gated = silu(rms_scale(lifted) * gain_enc)
        encoded = (lifted + conv(gated, 0)).astype(jnp.bfloat16).astype(jnp.float32)
        gated = silu(rms_scale(encoded) * gain_dec)
        skipped = lifted.astype(jnp.bfloat16).astype(jnp.float32)
        merged = encoded + conv(gated, 1) + skipped
        net_out = jnp.dot(
            silu(rms_scale(merged)),
            out_ref[...],
            precision=lax.Precision.HIGHEST,
            preferred_element_type=jnp.float32,
        )
        denoised = keep_state * state + keep_net * net_out
        return state + move * (state - denoised)

    result_ref[...] = lax.fori_loop(0, STEPS, one_step, state_ref[...])


def run_chain(coefs, state, means, lift, embed, kernels, gains, out_weight):
    vmem = pltpu.MemorySpace.VMEM
    return pl.pallas_call(
        chain_kernel,
        out_shape=jax.ShapeDtypeStruct(state.shape, jnp.float32),
        in_specs=[pl.BlockSpec(memory_space=pltpu.MemorySpace.SMEM)]
        + [pl.BlockSpec(memory_space=vmem)] * 7,
        out_specs=pl.BlockSpec(memory_space=vmem),
    )(coefs, state, means, lift, embed, kernels, gains, out_weight)


def step_coefficients(sigmas):
    sigma_now = sigmas[:-1]
    sigma_next = sigmas[1:]
    spread = sigma_now * sigma_now + DATA_VAR
    return jnp.stack(
        [
            lax.rsqrt(spread),
            jnp.log(sigma_now) / 4.0,
            DATA_VAR / spread,
            0.5 * sigma_now * lax.rsqrt(spread),
            (sigma_next - sigma_now) / sigma_now,
        ],
        axis=1,
    ).reshape(-1)


def to_lanes(fields, first_lane, lanes):
    batched, variables, pixels = fields.shape
    flat = jnp.transpose(fields, (0, 2, 1)).reshape(batched * pixels, variables)
    return jnp.pad(flat, ((0, 0), (first_lane, lanes - first_lane - variables)))


def make_body(routes):
    def body(
        start_noise,
        reg_means,
        hour_owner,
        member_tile,
        sigmas,
        lift_weight,
        noise_embed,
        section_conv,
        section_gain,
        out_weight,
    ):
        segment_index = lax.axis_index("segment")
        is_first = segment_index == 0
        half_hours = HOURS // lax.axis_size("segment")
        first_hour = segment_index * half_hours
        variables = start_noise.shape[2]
        pixels = start_noise.shape[3]
        channels = section_conv.shape[-1]

        swap = [(0, 1), (1, 0)]
        other_conv = lax.ppermute(section_conv, "segment", swap)
        other_gain = lax.ppermute(section_gain, "segment", swap)
        kernels = jnp.stack(
            [
                jnp.where(is_first, section_conv[0], other_conv[0]),
                jnp.where(is_first, other_conv[0], section_conv[0]),
            ]
        ).reshape(2, 9 * channels, channels)
        gains = jnp.stack(
            [
                jnp.where(is_first, section_gain[0], other_gain[0]),
                jnp.where(is_first, other_gain[0], section_gain[0]),
            ]
        ).astype(jnp.float32)

        owners = lax.dynamic_slice_in_dim(hour_owner, first_hour, half_hours, 0)
        mine = lax.dynamic_slice_in_dim(reg_means[0], first_hour, half_hours, 0)
        is_owner = lax.axis_index("member") == owners
        kept = jnp.where(is_owner[:, None, None, None], mine, 0).astype(mine.dtype)
        if [n for n, _, _ in routes] == [4, 4, 8]:
            means = targeted_mean(kept, member_tile[0], routes)
        else:
            arrived = broadcast_sum(kept, routes)
            means = lax.dynamic_index_in_dim(arrived, member_tile[0], 1, keepdims=False)

        noise = lax.dynamic_slice_in_dim(start_noise[0], first_hour, half_hours, 0)
        states = sigmas[0] * noise
        lift = jnp.pad(lift_weight, ((0, channels - 2 * variables), (0, 0)))
        out_pad = jnp.pad(out_weight, ((0, 0), (0, channels - variables)))
        finished = run_chain(
            step_coefficients(sigmas),
            to_lanes(states, 0, channels),
            to_lanes(means, variables, channels),
            lift,
            noise_embed[None, :],
            kernels,
            gains,
            out_pad,
        )
        finished = finished[:, :variables].reshape(half_hours, pixels, variables)
        return (means + jnp.transpose(finished, (0, 2, 1)))[:, None]

    return body


def solution(mesh):
    placed = (
        P("member", None, None, None),
        P("member", None, None, None, None),
        P(),
        P("member"),
        P(),
        P(),
        P(),
        P("segment", None, None, None),
        P("segment", None),
        P(),
    )
    return jax.shard_map(
        make_body(ring_routes(mesh)),
        mesh=mesh,
        in_specs=placed,
        out_specs=P("segment", "member", None, None),
        check_vma=False,
    )
```

```python
import numpy as np
import jax
import jax.numpy as jnp
from jax import lax
from jax.sharding import PartitionSpec as P
from jax.experimental import pallas as pl
from jax.experimental.pallas import tpu as pltpu

SIDE = 16
HOURS = 4
STEPS = 8


EPSILON = 1e-06
DATA_VAR = 0.25


def ring_routes(mesh):
    devices = np.asarray(mesh.devices)[:, 0]
    coords = [tuple(d.coords[:3]) for d in devices]
    where = {c: i for i, c in enumerate(coords)}
    sizes = [len({c[a] for c in coords}) for a in range(3)]
    axes = [a for a in sorted(range(3), key=lambda a: sizes[a]) if sizes[a] > 1]

    def shift_pairs(axis, distance):
        pairs = []
        for i, c in enumerate(coords):
            moved = list(c)
            moved[axis] = (c[axis] + distance) % sizes[axis]
            pairs.append((i, where[tuple(moved)]))
        return tuple(pairs)

    rings = []
    for axis in axes:
        n = sizes[axis]
        shifts = {d: shift_pairs(axis, d) for d in range(-n + 1, n) if d}
        position = tuple(c[axis] for c in coords)
        rings.append((n, shifts, position))
    return rings


def window_stages(n):
    if n & (n - 1):
        raise ValueError("ring size")
    if n == 2:
        return [(1,)]
    stages = [(1, -1, 2)]
    distance = 4
    while distance < n:
        stages.append((distance,))
        distance *= 2
    return stages


def broadcast_sum(block, rings):
    for n, shifts, _ in rings:
        for stage in window_stages(n):
            arrived = [lax.ppermute(block, "member", shifts[d]) for d in stage]
            for part in arrived:
                block = block + part
    return block


def reversed_pairs(pairs):
    return tuple((j, i) for i, j in pairs)


def broadcast_mean(kept, tile, rings):
    stages = [(shifts, stage) for n, shifts, _ in rings for stage in window_stages(n)]
    last_shifts, last_stage = stages[-1]
    if len(last_stage) != 1:
        block = broadcast_sum(kept, rings)
        return lax.dynamic_index_in_dim(block, tile, 1, keepdims=False)
    last_pairs = last_shifts[last_stage[0]]
    wanted = lax.ppermute(tile[None], "member", reversed_pairs(last_pairs))[0]
    block = kept
    for shifts, stage in stages[:-1]:
        arrived = [lax.ppermute(block, "member", shifts[d]) for d in stage]
        for part in arrived:
            block = block + part
    sent = lax.dynamic_index_in_dim(block, wanted, 1, keepdims=False)
    arrived = lax.ppermute(sent, "member", last_pairs)
    return lax.dynamic_index_in_dim(block, tile, 1, keepdims=False) + arrived


def rms_scale(values):
    return values * lax.rsqrt(jnp.mean(values * values, axis=-1, keepdims=True) + EPSILON)


def silu(values):
    return values / (1.0 + jnp.exp(-values))


def chain_kernel(coef_ref, state_ref, means_ref, lift_ref, embed_ref, conv_ref, gain_ref, out_ref, result_ref):
    rows, lanes = state_ref.shape
    pixel = lax.broadcasted_iota(jnp.int32, (rows, lanes), 0) % (SIDE * SIDE)
    row = pixel // SIDE
    col = pixel % SIDE
    row_ok = {a: (row + a >= 0) & (row + a < SIDE) for a in (-1, 1)}
    col_ok = {b: (col + b >= 0) & (col + b < SIDE) for b in (-1, 1)}

    def conv(gated, index):
        columns = {}
        for b in (-1, 0, 1):
            moved = gated
            if b:
                moved = jnp.where(col_ok[b], pltpu.roll(gated, (-b) % rows, 0), 0.0)
            columns[b] = moved
        windows = []
        for a in (-1, 0, 1):
            for b in (-1, 0, 1):
                moved = columns[b]
                if a == 1:
                    moved = jnp.concatenate([moved[SIDE:], moved[:SIDE]], axis=0)
                if a == -1:
                    moved = jnp.concatenate([moved[-SIDE:], moved[:-SIDE]], axis=0)
                if a:
                    moved = jnp.where(row_ok[a], moved, 0.0)
                windows.append(moved.astype(jnp.bfloat16))
        stacked = jnp.concatenate(windows, axis=1)
        return jnp.dot(stacked, conv_ref[index], preferred_element_type=jnp.float32)

    means = means_ref[...]
    embed = embed_ref[...]
    gain_enc = gain_ref[0:1, :]
    gain_dec = gain_ref[1:2, :]

    def one_step(step, state):
        scale_in = coef_ref[step * 5 + 0]
        level = coef_ref[step * 5 + 1]
        keep_state = coef_ref[step * 5 + 2]
        keep_net = coef_ref[step * 5 + 3]
        move = coef_ref[step * 5 + 4]
        inputs = state * scale_in + means
        lifted = jnp.dot(
            inputs, lift_ref[...], precision=lax.Precision.HIGHEST, preferred_element_type=jnp.float32
        )
        lifted = lifted + level * embed
        gated = silu(rms_scale(lifted) * gain_enc)
        encoded = (lifted + conv(gated, 0)).astype(jnp.bfloat16).astype(jnp.float32)
        gated = silu(rms_scale(encoded) * gain_dec)
        skipped = lifted.astype(jnp.bfloat16).astype(jnp.float32)
        merged = encoded + conv(gated, 1) + skipped
        net_out = jnp.dot(
            silu(rms_scale(merged)),
            out_ref[...],
            precision=lax.Precision.HIGHEST,
            preferred_element_type=jnp.float32,
        )
        denoised = keep_state * state + keep_net * net_out
        return state + move * (state - denoised)

    result_ref[...] = lax.fori_loop(0, STEPS, one_step, state_ref[...])


def run_chain(coefs, state, means, lift, embed, kernels, gains, out_weight):
    vmem = pltpu.MemorySpace.VMEM
    return pl.pallas_call(
        chain_kernel,
        out_shape=jax.ShapeDtypeStruct(state.shape, jnp.float32),
        in_specs=[pl.BlockSpec(memory_space=pltpu.MemorySpace.SMEM)]
        + [pl.BlockSpec(memory_space=vmem)] * 7,
        out_specs=pl.BlockSpec(memory_space=vmem),
    )(coefs, state, means, lift, embed, kernels, gains, out_weight)


def step_coefficients(sigmas):
    sigma_now = sigmas[:-1]
    sigma_next = sigmas[1:]
    spread = sigma_now * sigma_now + DATA_VAR
    return jnp.stack(
        [
            lax.rsqrt(spread),
            jnp.log(sigma_now) / 4.0,
            DATA_VAR / spread,
            0.5 * sigma_now * lax.rsqrt(spread),
            (sigma_next - sigma_now) / sigma_now,
        ],
        axis=1,
    ).reshape(-1)


def to_lanes(fields, first_lane, lanes):
    batched, variables, pixels = fields.shape
    flat = jnp.transpose(fields, (0, 2, 1)).reshape(batched * pixels, variables)
    return jnp.pad(flat, ((0, 0), (first_lane, lanes - first_lane - variables)))


def make_body(routes):
    def body(
        start_noise,
        reg_means,
        hour_owner,
        member_tile,
        sigmas,
        lift_weight,
        noise_embed,
        section_conv,
        section_gain,
        out_weight,
    ):
        segment_index = lax.axis_index("segment")
        is_first = segment_index == 0
        half_hours = HOURS // lax.axis_size("segment")
        first_hour = segment_index * half_hours
        variables = start_noise.shape[2]
        pixels = start_noise.shape[3]
        channels = section_conv.shape[-1]

        swap = [(0, 1), (1, 0)]
        other_conv = lax.ppermute(section_conv, "segment", swap)
        other_gain = lax.ppermute(section_gain, "segment", swap)
        kernels = jnp.stack(
            [
                jnp.where(is_first, section_conv[0], other_conv[0]),
                jnp.where(is_first, other_conv[0], section_conv[0]),
            ]
        ).reshape(2, 9 * channels, channels)
        gains = jnp.stack(
            [
                jnp.where(is_first, section_gain[0], other_gain[0]),
                jnp.where(is_first, other_gain[0], section_gain[0]),
            ]
        ).astype(jnp.float32)

        owners = lax.dynamic_slice_in_dim(hour_owner, first_hour, half_hours, 0)
        mine = lax.dynamic_slice_in_dim(reg_means[0], first_hour, half_hours, 0)
        is_owner = lax.axis_index("member") == owners
        kept = jnp.where(is_owner[:, None, None, None], mine, 0).astype(mine.dtype)
        means = broadcast_mean(kept, member_tile[0], routes)

        noise = lax.dynamic_slice_in_dim(start_noise[0], first_hour, half_hours, 0)
        states = sigmas[0] * noise
        lift = jnp.pad(lift_weight, ((0, channels - 2 * variables), (0, 0)))
        out_pad = jnp.pad(out_weight, ((0, 0), (0, channels - variables)))
        finished = run_chain(
            step_coefficients(sigmas),
            to_lanes(states, 0, channels),
            to_lanes(means, variables, channels),
            lift,
            noise_embed[None, :],
            kernels,
            gains,
            out_pad,
        )
        finished = finished[:, :variables].reshape(half_hours, pixels, variables)
        return (means + jnp.transpose(finished, (0, 2, 1)))[:, None]

    return body


def solution(mesh):
    placed = (
        P("member", None, None, None),
        P("member", None, None, None, None),
        P(),
        P("member"),
        P(),
        P(),
        P(),
        P("segment", None, None, None),
        P("segment", None),
        P(),
    )
    return jax.shard_map(
        make_body(ring_routes(mesh)),
        mesh=mesh,
        in_specs=placed,
        out_specs=P("segment", "member", None, None),
        check_vma=False,
    )
```

```python
import numpy as np
import jax
import jax.numpy as jnp
from jax import lax
from jax.sharding import PartitionSpec as P
from jax.experimental import pallas as pl
from jax.experimental.pallas import tpu as pltpu

SIDE = 16
HOURS = 4
STEPS = 8


EPSILON = 1e-06
DATA_VAR = 0.25


def ring_routes(mesh):
    devices = np.asarray(mesh.devices)[:, 0]
    coords = [tuple(d.coords[:3]) for d in devices]
    where = {c: i for i, c in enumerate(coords)}
    sizes = [len({c[a] for c in coords}) for a in range(3)]
    axes = [a for a in sorted(range(3), key=lambda a: sizes[a]) if sizes[a] > 1]

    def shift_pairs(axis, distance):
        pairs = []
        for i, c in enumerate(coords):
            moved = list(c)
            moved[axis] = (c[axis] + distance) % sizes[axis]
            pairs.append((i, where[tuple(moved)]))
        return tuple(pairs)

    rings = []
    for axis in axes:
        n = sizes[axis]
        shifts = {d: shift_pairs(axis, d) for d in range(-n + 1, n) if d}
        position = tuple(c[axis] for c in coords)
        rings.append((n, shifts, position))
    return rings


def window_stages(n):
    if n & (n - 1):
        raise ValueError("ring size")
    if n == 2:
        return [(1,)]
    stages = [(1, -1, 2)]
    distance = 4
    while distance < n:
        stages.append((distance,))
        distance *= 2
    return stages


def broadcast_sum(block, rings):
    for n, shifts, _ in rings:
        for stage in window_stages(n):
            arrived = [lax.ppermute(block, "member", shifts[d]) for d in stage]
            for part in arrived:
                block = block + part
    return block


def reversed_pairs(pairs):
    return tuple((j, i) for i, j in pairs)


def broadcast_mean(kept, tile, rings):
    stages = [(shifts, stage) for n, shifts, _ in rings for stage in window_stages(n)]
    last_shifts, last_stage = stages[-1]
    if len(last_stage) != 1:
        block = broadcast_sum(kept, rings)
        return lax.dynamic_index_in_dim(block, tile, 1, keepdims=False)
    last_pairs = last_shifts[last_stage[0]]
    wanted = lax.ppermute(tile[None], "member", reversed_pairs(last_pairs))[0]
    block = kept
    for shifts, stage in stages[:-1]:
        arrived = [lax.ppermute(block, "member", shifts[d]) for d in stage]
        for part in arrived:
            block = block + part
    sent = lax.dynamic_index_in_dim(block, wanted, 1, keepdims=False)
    arrived = lax.ppermute(sent, "member", last_pairs)
    return lax.dynamic_index_in_dim(block, tile, 1, keepdims=False) + arrived


def rms_scale(values):
    return values * lax.rsqrt(jnp.mean(values * values, axis=-1, keepdims=True) + EPSILON)


def silu(values):
    return values / (1.0 + jnp.exp(-values))


def chain_kernel(coef_ref, state_ref, means_ref, lift_ref, embed_ref, conv_ref, gain_ref, out_ref, result_ref):
    rows, lanes = state_ref.shape
    pixel = lax.broadcasted_iota(jnp.int32, (rows, lanes), 0) % (SIDE * SIDE)
    col = pixel % SIDE
    col_ok = {b: (col + b >= 0) & (col + b < SIDE) for b in (-1, 1)}
    tiles = rows // (SIDE * SIDE)
    zero_row = jnp.zeros((SIDE, lanes), jnp.bfloat16)

    def shift_rows(moved, a):
        parts = []
        for t in range(tiles):
            tile = moved[t * SIDE * SIDE : (t + 1) * SIDE * SIDE]
            if a == 1:
                parts += [tile[SIDE:], zero_row]
            else:
                parts += [zero_row, tile[:-SIDE]]
        return jnp.concatenate(parts, axis=0)

    def conv(gated, index):
        columns = {}
        for b in (-1, 0, 1):
            moved = gated
            if b:
                moved = jnp.where(col_ok[b], pltpu.roll(gated, (-b) % rows, 0), 0.0)
            columns[b] = moved.astype(jnp.bfloat16)
        windows = []
        for a in (-1, 0, 1):
            for b in (-1, 0, 1):
                windows.append(columns[b] if a == 0 else shift_rows(columns[b], a))
        stacked = jnp.concatenate(windows, axis=1)
        return jnp.dot(stacked, conv_ref[index], preferred_element_type=jnp.float32)

    means = means_ref[...]
    embed = embed_ref[...]
    gain_enc = gain_ref[0:1, :]
    gain_dec = gain_ref[1:2, :]

    def one_step(step, state):
        scale_in = coef_ref[step * 5 + 0]
        level = coef_ref[step * 5 + 1]
        keep_state = coef_ref[step * 5 + 2]
        keep_net = coef_ref[step * 5 + 3]
        move = coef_ref[step * 5 + 4]
        inputs = state * scale_in + means
        lifted = jnp.dot(
            inputs, lift_ref[...], precision=lax.Precision.HIGHEST, preferred_element_type=jnp.float32
        )
        lifted = lifted + level * embed
        gated = silu(rms_scale(lifted) * gain_enc)
        encoded = (lifted + conv(gated, 0)).astype(jnp.bfloat16).astype(jnp.float32)
        gated = silu(rms_scale(encoded) * gain_dec)
        skipped = lifted.astype(jnp.bfloat16).astype(jnp.float32)
        merged = encoded + conv(gated, 1) + skipped
        net_out = jnp.dot(
            silu(rms_scale(merged)),
            out_ref[...],
            precision=lax.Precision.HIGHEST,
            preferred_element_type=jnp.float32,
        )
        denoised = keep_state * state + keep_net * net_out
        return state + move * (state - denoised)

    result_ref[...] = lax.fori_loop(0, STEPS, one_step, state_ref[...])


def run_chain(coefs, state, means, lift, embed, kernels, gains, out_weight):
    vmem = pltpu.MemorySpace.VMEM
    return pl.pallas_call(
        chain_kernel,
        out_shape=jax.ShapeDtypeStruct(state.shape, jnp.float32),
        in_specs=[pl.BlockSpec(memory_space=pltpu.MemorySpace.SMEM)]
        + [pl.BlockSpec(memory_space=vmem)] * 7,
        out_specs=pl.BlockSpec(memory_space=vmem),
    )(coefs, state, means, lift, embed, kernels, gains, out_weight)


def step_coefficients(sigmas):
    sigma_now = sigmas[:-1]
    sigma_next = sigmas[1:]
    spread = sigma_now * sigma_now + DATA_VAR
    return jnp.stack(
        [
            lax.rsqrt(spread),
            jnp.log(sigma_now) / 4.0,
            DATA_VAR / spread,
            0.5 * sigma_now * lax.rsqrt(spread),
            (sigma_next - sigma_now) / sigma_now,
        ],
        axis=1,
    ).reshape(-1)


def to_lanes(fields, first_lane, lanes):
    batched, variables, pixels = fields.shape
    flat = jnp.transpose(fields, (0, 2, 1)).reshape(batched * pixels, variables)
    return jnp.pad(flat, ((0, 0), (first_lane, lanes - first_lane - variables)))


def make_body(routes):
    def body(
        start_noise,
        reg_means,
        hour_owner,
        member_tile,
        sigmas,
        lift_weight,
        noise_embed,
        section_conv,
        section_gain,
        out_weight,
    ):
        segment_index = lax.axis_index("segment")
        is_first = segment_index == 0
        half_hours = HOURS // lax.axis_size("segment")
        first_hour = segment_index * half_hours
        variables = start_noise.shape[2]
        pixels = start_noise.shape[3]
        channels = section_conv.shape[-1]

        swap = [(0, 1), (1, 0)]
        other_conv = lax.ppermute(section_conv, "segment", swap)
        other_gain = lax.ppermute(section_gain, "segment", swap)
        kernels = jnp.stack(
            [
                jnp.where(is_first, section_conv[0], other_conv[0]),
                jnp.where(is_first, other_conv[0], section_conv[0]),
            ]
        ).reshape(2, 9 * channels, channels)
        gains = jnp.stack(
            [
                jnp.where(is_first, section_gain[0], other_gain[0]),
                jnp.where(is_first, other_gain[0], section_gain[0]),
            ]
        ).astype(jnp.float32)

        owners = lax.dynamic_slice_in_dim(hour_owner, first_hour, half_hours, 0)
        mine = lax.dynamic_slice_in_dim(reg_means[0], first_hour, half_hours, 0)
        is_owner = lax.axis_index("member") == owners
        kept = jnp.where(is_owner[:, None, None, None], mine, 0).astype(mine.dtype)
        means = broadcast_mean(kept, member_tile[0], routes)

        noise = lax.dynamic_slice_in_dim(start_noise[0], first_hour, half_hours, 0)
        states = sigmas[0] * noise
        lift = jnp.pad(lift_weight, ((0, channels - 2 * variables), (0, 0)))
        out_pad = jnp.pad(out_weight, ((0, 0), (0, channels - variables)))
        finished = run_chain(
            step_coefficients(sigmas),
            to_lanes(states, 0, channels),
            to_lanes(means, variables, channels),
            lift,
            noise_embed[None, :],
            kernels,
            gains,
            out_pad,
        )
        finished = finished[:, :variables].reshape(half_hours, pixels, variables)
        return (means + jnp.transpose(finished, (0, 2, 1)))[:, None]

    return body


def solution(mesh):
    placed = (
        P("member", None, None, None),
        P("member", None, None, None, None),
        P(),
        P("member"),
        P(),
        P(),
        P(),
        P("segment", None, None, None),
        P("segment", None),
        P(),
    )
    return jax.shard_map(
        make_body(ring_routes(mesh)),
        mesh=mesh,
        in_specs=placed,
        out_specs=P("segment", "member", None, None),
        check_vma=False,
    )
```

```python
import numpy as np
import jax
import jax.numpy as jnp
from jax import lax
from jax.sharding import PartitionSpec as P
from jax.experimental import pallas as pl
from jax.experimental.pallas import tpu as pltpu

SIDE = 16
HOURS = 4
STEPS = 8


EPSILON = 1e-06
DATA_VAR = 0.25


def ring_routes(mesh):
    devices = np.asarray(mesh.devices)[:, 0]
    coords = [tuple(d.coords[:3]) for d in devices]
    where = {c: i for i, c in enumerate(coords)}
    sizes = [len({c[a] for c in coords}) for a in range(3)]
    axes = [a for a in sorted(range(3), key=lambda a: sizes[a]) if sizes[a] > 1]

    def shift_pairs(axis, distance):
        pairs = []
        for i, c in enumerate(coords):
            moved = list(c)
            moved[axis] = (c[axis] + distance) % sizes[axis]
            pairs.append((i, where[tuple(moved)]))
        return tuple(pairs)

    rings = []
    for axis in axes:
        n = sizes[axis]
        shifts = {d: shift_pairs(axis, d) for d in range(-n + 1, n) if d}
        position = tuple(c[axis] for c in coords)
        rings.append((n, shifts, position))
    return rings


def window_stages(n):
    if n & (n - 1):
        raise ValueError("ring size")
    if n == 2:
        return [(1,)]
    stages = [(1, -1, 2)]
    distance = 4
    while distance < n:
        stages.append((distance,))
        distance *= 2
    return stages


def broadcast_sum(block, rings):
    for n, shifts, _ in rings:
        for stage in window_stages(n):
            arrived = [lax.ppermute(block, "member", shifts[d]) for d in stage]
            for part in arrived:
                block = block + part
    return block


def reversed_pairs(pairs):
    return tuple((j, i) for i, j in pairs)


def broadcast_mean(kept, tile, rings):
    size_z, shifts_z, position_z = rings[-1]
    if size_z != 8:
        block = broadcast_sum(kept, rings)
        return lax.dynamic_index_in_dim(block, tile, 1, keepdims=False)
    at_z = jnp.asarray(position_z, jnp.int32)[lax.axis_index("member")]
    slots = jnp.arange(size_z, dtype=jnp.int32)
    tiles_z = jnp.where(slots == at_z, tile, 0)
    for d in (1, 2, 4):
        tiles_z = tiles_z + lax.ppermute(tiles_z, "member", shifts_z[d])

    block = broadcast_sum(kept, rings[:-1])

    def served(first):
        picked = jnp.stack([first % size_z, (first + size_z // 2) % size_z])
        return jnp.take(block, jnp.take(tiles_z, picked), axis=1, mode="clip")

    arrived = [lax.ppermute(served(at_z + d), "member", shifts_z[d]) for d in (1, -1, 2)]
    block = served(at_z)
    for part in arrived:
        block = block + part
    arrived = lax.ppermute(block[:, 1], "member", shifts_z[size_z // 2])
    return block[:, 0] + arrived


def rms_scale(values):
    return values * lax.rsqrt(jnp.mean(values * values, axis=-1, keepdims=True) + EPSILON)


def silu(values):
    return values / (1.0 + jnp.exp(-values))


def chain_kernel(coef_ref, state_ref, means_ref, lift_ref, embed_ref, conv_ref, gain_ref, out_ref, result_ref):
    rows, lanes = state_ref.shape
    pixel = lax.broadcasted_iota(jnp.int32, (rows, lanes), 0) % (SIDE * SIDE)
    col = pixel % SIDE
    col_ok = {b: (col + b >= 0) & (col + b < SIDE) for b in (-1, 1)}
    tiles = rows // (SIDE * SIDE)
    zero_row = jnp.zeros((SIDE, lanes), jnp.bfloat16)

    def shift_rows(moved, a):
        parts = []
        for t in range(tiles):
            tile = moved[t * SIDE * SIDE : (t + 1) * SIDE * SIDE]
            if a == 1:
                parts += [tile[SIDE:], zero_row]
            else:
                parts += [zero_row, tile[:-SIDE]]
        return jnp.concatenate(parts, axis=0)

    def conv(gated, index):
        columns = {}
        for b in (-1, 0, 1):
            moved = gated
            if b:
                moved = jnp.where(col_ok[b], pltpu.roll(gated, (-b) % rows, 0), 0.0)
            columns[b] = moved.astype(jnp.bfloat16)
        windows = []
        for a in (-1, 0, 1):
            for b in (-1, 0, 1):
                windows.append(columns[b] if a == 0 else shift_rows(columns[b], a))
        stacked = jnp.concatenate(windows, axis=1)
        return jnp.dot(stacked, conv_ref[index], preferred_element_type=jnp.float32)

    means = means_ref[...]
    embed = embed_ref[...]
    gain_enc = gain_ref[0:1, :]
    gain_dec = gain_ref[1:2, :]

    def one_step(step, state):
        scale_in = coef_ref[step * 5 + 0]
        level = coef_ref[step * 5 + 1]
        keep_state = coef_ref[step * 5 + 2]
        keep_net = coef_ref[step * 5 + 3]
        move = coef_ref[step * 5 + 4]
        inputs = state * scale_in + means
        lifted = jnp.dot(
            inputs, lift_ref[...], precision=lax.Precision.HIGHEST, preferred_element_type=jnp.float32
        )
        lifted = lifted + level * embed
        gated = silu(rms_scale(lifted) * gain_enc)
        encoded = (lifted + conv(gated, 0)).astype(jnp.bfloat16).astype(jnp.float32)
        gated = silu(rms_scale(encoded) * gain_dec)
        skipped = lifted.astype(jnp.bfloat16).astype(jnp.float32)
        merged = encoded + conv(gated, 1) + skipped
        net_out = jnp.dot(
            silu(rms_scale(merged)),
            out_ref[...],
            precision=lax.Precision.HIGHEST,
            preferred_element_type=jnp.float32,
        )
        denoised = keep_state * state + keep_net * net_out
        return state + move * (state - denoised)

    result_ref[...] = lax.fori_loop(0, STEPS, one_step, state_ref[...])


def run_chain(coefs, state, means, lift, embed, kernels, gains, out_weight):
    vmem = pltpu.MemorySpace.VMEM
    return pl.pallas_call(
        chain_kernel,
        out_shape=jax.ShapeDtypeStruct(state.shape, jnp.float32),
        in_specs=[pl.BlockSpec(memory_space=pltpu.MemorySpace.SMEM)]
        + [pl.BlockSpec(memory_space=vmem)] * 7,
        out_specs=pl.BlockSpec(memory_space=vmem),
    )(coefs, state, means, lift, embed, kernels, gains, out_weight)


def step_coefficients(sigmas):
    sigma_now = sigmas[:-1]
    sigma_next = sigmas[1:]
    spread = sigma_now * sigma_now + DATA_VAR
    return jnp.stack(
        [
            lax.rsqrt(spread),
            jnp.log(sigma_now) / 4.0,
            DATA_VAR / spread,
            0.5 * sigma_now * lax.rsqrt(spread),
            (sigma_next - sigma_now) / sigma_now,
        ],
        axis=1,
    ).reshape(-1)


def to_lanes(fields, first_lane, lanes):
    batched, variables, pixels = fields.shape
    flat = jnp.transpose(fields, (0, 2, 1)).reshape(batched * pixels, variables)
    return jnp.pad(flat, ((0, 0), (first_lane, lanes - first_lane - variables)))


def make_body(routes):
    def body(
        start_noise,
        reg_means,
        hour_owner,
        member_tile,
        sigmas,
        lift_weight,
        noise_embed,
        section_conv,
        section_gain,
        out_weight,
    ):
        segment_index = lax.axis_index("segment")
        is_first = segment_index == 0
        half_hours = HOURS // lax.axis_size("segment")
        first_hour = segment_index * half_hours
        variables = start_noise.shape[2]
        pixels = start_noise.shape[3]
        channels = section_conv.shape[-1]

        swap = [(0, 1), (1, 0)]
        other_conv = lax.ppermute(section_conv, "segment", swap)
        other_gain = lax.ppermute(section_gain, "segment", swap)
        kernels = jnp.stack(
            [
                jnp.where(is_first, section_conv[0], other_conv[0]),
                jnp.where(is_first, other_conv[0], section_conv[0]),
            ]
        ).reshape(2, 9 * channels, channels)
        gains = jnp.stack(
            [
                jnp.where(is_first, section_gain[0], other_gain[0]),
                jnp.where(is_first, other_gain[0], section_gain[0]),
            ]
        ).astype(jnp.float32)

        owners = lax.dynamic_slice_in_dim(hour_owner, first_hour, half_hours, 0)
        mine = lax.dynamic_slice_in_dim(reg_means[0], first_hour, half_hours, 0)
        is_owner = lax.axis_index("member") == owners
        kept = jnp.where(is_owner[:, None, None, None], mine, 0).astype(mine.dtype)
        means = broadcast_mean(kept, member_tile[0], routes)

        noise = lax.dynamic_slice_in_dim(start_noise[0], first_hour, half_hours, 0)
        states = sigmas[0] * noise
        lift = jnp.pad(lift_weight, ((0, channels - 2 * variables), (0, 0)))
        out_pad = jnp.pad(out_weight, ((0, 0), (0, channels - variables)))
        finished = run_chain(
            step_coefficients(sigmas),
            to_lanes(states, 0, channels),
            to_lanes(means, variables, channels),
            lift,
            noise_embed[None, :],
            kernels,
            gains,
            out_pad,
        )
        finished = finished[:, :variables].reshape(half_hours, pixels, variables)
        return (means + jnp.transpose(finished, (0, 2, 1)))[:, None]

    return body


def solution(mesh):
    placed = (
        P("member", None, None, None),
        P("member", None, None, None, None),
        P(),
        P("member"),
        P(),
        P(),
        P(),
        P("segment", None, None, None),
        P("segment", None),
        P(),
    )
    return jax.shard_map(
        make_body(ring_routes(mesh)),
        mesh=mesh,
        in_specs=placed,
        out_specs=P("segment", "member", None, None),
        check_vma=False,
    )
```

```python
import numpy as np
import jax
import jax.numpy as jnp
from jax import lax
from jax.sharding import PartitionSpec as P
from jax.experimental import pallas as pl
from jax.experimental.pallas import tpu as pltpu

SIDE = 16
HOURS = 4
STEPS = 8


EPSILON = 1e-06
DATA_VAR = 0.25


def ring_routes(mesh):
    devices = np.asarray(mesh.devices)[:, 0]
    coords = [tuple(d.coords[:3]) for d in devices]
    where = {c: i for i, c in enumerate(coords)}
    sizes = [len({c[a] for c in coords}) for a in range(3)]
    axes = [a for a in sorted(range(3), key=lambda a: sizes[a]) if sizes[a] > 1]

    def shift_pairs(axis, distance):
        pairs = []
        for i, c in enumerate(coords):
            moved = list(c)
            moved[axis] = (c[axis] + distance) % sizes[axis]
            pairs.append((i, where[tuple(moved)]))
        return tuple(pairs)

    rings = []
    for axis in axes:
        n = sizes[axis]
        shifts = {d: shift_pairs(axis, d) for d in range(-n + 1, n) if d}
        position = tuple(c[axis] for c in coords)
        rings.append((n, shifts, position))
    return rings


def window_stages(n):
    if n & (n - 1):
        raise ValueError("ring size")
    if n == 2:
        return [(1,)]
    stages = [(1, -1, 2)]
    distance = 4
    while distance < n:
        stages.append((distance,))
        distance *= 2
    return stages


def broadcast_sum(block, rings):
    for n, shifts, _ in rings:
        for stage in window_stages(n):
            arrived = [lax.ppermute(block, "member", shifts[d]) for d in stage]
            for part in arrived:
                block = block + part
    return block


def reversed_pairs(pairs):
    return tuple((j, i) for i, j in pairs)


def broadcast_mean(kept, tile, rings):
    size_z, shifts_z, _ = rings[-1]
    if size_z < 4 or size_z % 2:
        block = broadcast_sum(kept, rings)
        return lax.dynamic_index_in_dim(block, tile, 1, keepdims=False)
    far = range(2, size_z, 2)
    wanted = {
        d: lax.ppermute(tile[None], "member", reversed_pairs(shifts_z[d]))[0] for d in far
    }
    block = broadcast_sum(kept, rings[:-1])
    block = block + lax.ppermute(block, "member", shifts_z[1])
    arrived = [
        lax.ppermute(
            lax.dynamic_index_in_dim(block, wanted[d], 1, keepdims=False), "member", shifts_z[d]
        )
        for d in far
    ]
    mean = lax.dynamic_index_in_dim(block, tile, 1, keepdims=False)
    for part in arrived:
        mean = mean + part
    return mean


def rms_scale(values):
    return values * lax.rsqrt(jnp.mean(values * values, axis=-1, keepdims=True) + EPSILON)


def silu(values):
    return values / (1.0 + jnp.exp(-values))


def chain_kernel(coef_ref, state_ref, means_ref, lift_ref, embed_ref, conv_ref, gain_ref, out_ref, result_ref):
    rows, lanes = state_ref.shape
    pixel = lax.broadcasted_iota(jnp.int32, (rows, lanes), 0) % (SIDE * SIDE)
    col = pixel % SIDE
    col_ok = {b: (col + b >= 0) & (col + b < SIDE) for b in (-1, 1)}
    tiles = rows // (SIDE * SIDE)
    zero_row = jnp.zeros((SIDE, lanes), jnp.bfloat16)

    def shift_rows(moved, a):
        parts = []
        for t in range(tiles):
            tile = moved[t * SIDE * SIDE : (t + 1) * SIDE * SIDE]
            if a == 1:
                parts += [tile[SIDE:], zero_row]
            else:
                parts += [zero_row, tile[:-SIDE]]
        return jnp.concatenate(parts, axis=0)

    def conv(gated, index):
        columns = {}
        for b in (-1, 0, 1):
            moved = gated
            if b:
                moved = jnp.where(col_ok[b], pltpu.roll(gated, (-b) % rows, 0), 0.0)
            columns[b] = moved.astype(jnp.bfloat16)
        windows = []
        for a in (-1, 0, 1):
            for b in (-1, 0, 1):
                windows.append(columns[b] if a == 0 else shift_rows(columns[b], a))
        stacked = jnp.concatenate(windows, axis=1)
        return jnp.dot(stacked, conv_ref[index], preferred_element_type=jnp.float32)

    means = means_ref[...]
    embed = embed_ref[...]
    gain_enc = gain_ref[0:1, :]
    gain_dec = gain_ref[1:2, :]

    def one_step(step, state):
        scale_in = coef_ref[step * 5 + 0]
        level = coef_ref[step * 5 + 1]
        keep_state = coef_ref[step * 5 + 2]
        keep_net = coef_ref[step * 5 + 3]
        move = coef_ref[step * 5 + 4]
        inputs = state * scale_in + means
        lifted = jnp.dot(
            inputs, lift_ref[...], precision=lax.Precision.HIGHEST, preferred_element_type=jnp.float32
        )
        lifted = lifted + level * embed
        gated = silu(rms_scale(lifted) * gain_enc)
        encoded = (lifted + conv(gated, 0)).astype(jnp.bfloat16).astype(jnp.float32)
        gated = silu(rms_scale(encoded) * gain_dec)
        skipped = lifted.astype(jnp.bfloat16).astype(jnp.float32)
        merged = encoded + conv(gated, 1) + skipped
        net_out = jnp.dot(
            silu(rms_scale(merged)),
            out_ref[...],
            precision=lax.Precision.HIGHEST,
            preferred_element_type=jnp.float32,
        )
        denoised = keep_state * state + keep_net * net_out
        return state + move * (state - denoised)

    result_ref[...] = lax.fori_loop(0, STEPS, one_step, state_ref[...])


def run_chain(coefs, state, means, lift, embed, kernels, gains, out_weight):
    vmem = pltpu.MemorySpace.VMEM
    return pl.pallas_call(
        chain_kernel,
        out_shape=jax.ShapeDtypeStruct(state.shape, jnp.float32),
        in_specs=[pl.BlockSpec(memory_space=pltpu.MemorySpace.SMEM)]
        + [pl.BlockSpec(memory_space=vmem)] * 7,
        out_specs=pl.BlockSpec(memory_space=vmem),
    )(coefs, state, means, lift, embed, kernels, gains, out_weight)


def step_coefficients(sigmas):
    sigma_now = sigmas[:-1]
    sigma_next = sigmas[1:]
    spread = sigma_now * sigma_now + DATA_VAR
    return jnp.stack(
        [
            lax.rsqrt(spread),
            jnp.log(sigma_now) / 4.0,
            DATA_VAR / spread,
            0.5 * sigma_now * lax.rsqrt(spread),
            (sigma_next - sigma_now) / sigma_now,
        ],
        axis=1,
    ).reshape(-1)


def to_lanes(fields, first_lane, lanes):
    batched, variables, pixels = fields.shape
    flat = jnp.transpose(fields, (0, 2, 1)).reshape(batched * pixels, variables)
    return jnp.pad(flat, ((0, 0), (first_lane, lanes - first_lane - variables)))


def make_body(routes):
    def body(
        start_noise,
        reg_means,
        hour_owner,
        member_tile,
        sigmas,
        lift_weight,
        noise_embed,
        section_conv,
        section_gain,
        out_weight,
    ):
        segment_index = lax.axis_index("segment")
        is_first = segment_index == 0
        half_hours = HOURS // lax.axis_size("segment")
        first_hour = segment_index * half_hours
        variables = start_noise.shape[2]
        pixels = start_noise.shape[3]
        channels = section_conv.shape[-1]

        swap = [(0, 1), (1, 0)]
        other_conv = lax.ppermute(section_conv, "segment", swap)
        other_gain = lax.ppermute(section_gain, "segment", swap)
        kernels = jnp.stack(
            [
                jnp.where(is_first, section_conv[0], other_conv[0]),
                jnp.where(is_first, other_conv[0], section_conv[0]),
            ]
        ).reshape(2, 9 * channels, channels)
        gains = jnp.stack(
            [
                jnp.where(is_first, section_gain[0], other_gain[0]),
                jnp.where(is_first, other_gain[0], section_gain[0]),
            ]
        ).astype(jnp.float32)

        owners = lax.dynamic_slice_in_dim(hour_owner, first_hour, half_hours, 0)
        mine = lax.dynamic_slice_in_dim(reg_means[0], first_hour, half_hours, 0)
        is_owner = lax.axis_index("member") == owners
        kept = jnp.where(is_owner[:, None, None, None], mine, 0).astype(mine.dtype)
        means = broadcast_mean(kept, member_tile[0], routes)

        noise = lax.dynamic_slice_in_dim(start_noise[0], first_hour, half_hours, 0)
        states = sigmas[0] * noise
        lift = jnp.pad(lift_weight, ((0, channels - 2 * variables), (0, 0)))
        out_pad = jnp.pad(out_weight, ((0, 0), (0, channels - variables)))
        finished = run_chain(
            step_coefficients(sigmas),
            to_lanes(states, 0, channels),
            to_lanes(means, variables, channels),
            lift,
            noise_embed[None, :],
            kernels,
            gains,
            out_pad,
        )
        finished = finished[:, :variables].reshape(half_hours, pixels, variables)
        return (means + jnp.transpose(finished, (0, 2, 1)))[:, None]

    return body


def solution(mesh):
    placed = (
        P("member", None, None, None),
        P("member", None, None, None, None),
        P(),
        P("member"),
        P(),
        P(),
        P(),
        P("segment", None, None, None),
        P("segment", None),
        P(),
    )
    return jax.shard_map(
        make_body(ring_routes(mesh)),
        mesh=mesh,
        in_specs=placed,
        out_specs=P("segment", "member", None, None),
        check_vma=False,
    )
```

```python
import numpy as np
import jax
import jax.numpy as jnp
from jax import lax
from jax.sharding import PartitionSpec as P
from jax.experimental import pallas as pl
from jax.experimental.pallas import tpu as pltpu

SIDE = 16
HOURS = 4
STEPS = 8


EPSILON = 1e-06
DATA_VAR = 0.25


def ring_routes(mesh):
    devices = np.asarray(mesh.devices)[:, 0]
    coords = [tuple(d.coords[:3]) for d in devices]
    where = {c: i for i, c in enumerate(coords)}
    sizes = [len({c[a] for c in coords}) for a in range(3)]
    axes = [a for a in sorted(range(3), key=lambda a: sizes[a]) if sizes[a] > 1]

    def shift_pairs(axis, distance):
        pairs = []
        for i, c in enumerate(coords):
            moved = list(c)
            moved[axis] = (c[axis] + distance) % sizes[axis]
            pairs.append((i, where[tuple(moved)]))
        return tuple(pairs)

    rings = []
    for axis in axes:
        n = sizes[axis]
        shifts = {d: shift_pairs(axis, d) for d in range(-n + 1, n) if d}
        position = tuple(c[axis] for c in coords)
        rings.append((n, shifts, position))
    return rings


def window_stages(n):
    if n & (n - 1):
        raise ValueError("ring size")
    if n == 2:
        return [(1,)]
    stages = [(1, -1, 2)]
    distance = 4
    while distance < n:
        stages.append((distance,))
        distance *= 2
    return stages


def broadcast_sum(block, rings):
    for n, shifts, _ in rings:
        for stage in window_stages(n):
            arrived = [lax.ppermute(block, "member", shifts[d]) for d in stage]
            for part in arrived:
                block = block + part
    return block


def reversed_pairs(pairs):
    return tuple((j, i) for i, j in pairs)


def broadcast_mean(kept, tile, rings):
    size_z, shifts_z, _ = rings[-1]
    if size_z < 4 or size_z % 2:
        block = broadcast_sum(kept, rings)
        return lax.dynamic_index_in_dim(block, tile, 1, keepdims=False)
    far = range(2, size_z, 2)
    wanted = {
        d: lax.ppermute(tile[None], "member", reversed_pairs(shifts_z[d]))[0] for d in far
    }
    block = broadcast_sum(kept, rings[:-1])
    half = block.shape[0] // 2
    if half:
        up = lax.ppermute(block[:half], "member", shifts_z[1])
        down = lax.ppermute(block[half:], "member", shifts_z[-1])
        block = block + jnp.concatenate([up, down], axis=0)
    else:
        block = block + lax.ppermute(block, "member", shifts_z[1])
    arrived = [
        lax.ppermute(
            lax.dynamic_index_in_dim(block, wanted[d], 1, keepdims=False), "member", shifts_z[d]
        )
        for d in far
    ]
    mean = lax.dynamic_index_in_dim(block, tile, 1, keepdims=False)
    for part in arrived:
        mean = mean + part
    return mean


def rms_scale(values):
    return values * lax.rsqrt(jnp.mean(values * values, axis=-1, keepdims=True) + EPSILON)


def silu(values):
    return values / (1.0 + jnp.exp(-values))


def chain_kernel(coef_ref, state_ref, means_ref, lift_ref, embed_ref, conv_ref, gain_ref, out_ref, result_ref):
    rows, lanes = state_ref.shape
    pixel = lax.broadcasted_iota(jnp.int32, (rows, lanes), 0) % (SIDE * SIDE)
    col = pixel % SIDE
    col_ok = {b: (col + b >= 0) & (col + b < SIDE) for b in (-1, 1)}
    tiles = rows // (SIDE * SIDE)
    zero_row = jnp.zeros((SIDE, lanes), jnp.bfloat16)

    def shift_rows(moved, a):
        parts = []
        for t in range(tiles):
            tile = moved[t * SIDE * SIDE : (t + 1) * SIDE * SIDE]
            if a == 1:
                parts += [tile[SIDE:], zero_row]
            else:
                parts += [zero_row, tile[:-SIDE]]
        return jnp.concatenate(parts, axis=0)

    def conv(gated, index):
        columns = {}
        for b in (-1, 0, 1):
            moved = gated
            if b:
                moved = jnp.where(col_ok[b], pltpu.roll(gated, (-b) % rows, 0), 0.0)
            columns[b] = moved.astype(jnp.bfloat16)
        windows = []
        for a in (-1, 0, 1):
            for b in (-1, 0, 1):
                windows.append(columns[b] if a == 0 else shift_rows(columns[b], a))
        stacked = jnp.concatenate(windows, axis=1)
        return jnp.dot(stacked, conv_ref[index], preferred_element_type=jnp.float32)

    means = means_ref[...]
    embed = embed_ref[...]
    gain_enc = gain_ref[0:1, :]
    gain_dec = gain_ref[1:2, :]

    def one_step(step, state):
        scale_in = coef_ref[step * 5 + 0]
        level = coef_ref[step * 5 + 1]
        keep_state = coef_ref[step * 5 + 2]
        keep_net = coef_ref[step * 5 + 3]
        move = coef_ref[step * 5 + 4]
        inputs = state * scale_in + means
        lifted = jnp.dot(
            inputs, lift_ref[...], precision=lax.Precision.HIGHEST, preferred_element_type=jnp.float32
        )
        lifted = lifted + level * embed
        gated = silu(rms_scale(lifted) * gain_enc)
        encoded = (lifted + conv(gated, 0)).astype(jnp.bfloat16).astype(jnp.float32)
        gated = silu(rms_scale(encoded) * gain_dec)
        skipped = lifted.astype(jnp.bfloat16).astype(jnp.float32)
        merged = encoded + conv(gated, 1) + skipped
        net_out = jnp.dot(
            silu(rms_scale(merged)),
            out_ref[...],
            precision=lax.Precision.HIGHEST,
            preferred_element_type=jnp.float32,
        )
        denoised = keep_state * state + keep_net * net_out
        return state + move * (state - denoised)

    result_ref[...] = lax.fori_loop(0, STEPS, one_step, state_ref[...])


def run_chain(coefs, state, means, lift, embed, kernels, gains, out_weight):
    vmem = pltpu.MemorySpace.VMEM
    return pl.pallas_call(
        chain_kernel,
        out_shape=jax.ShapeDtypeStruct(state.shape, jnp.float32),
        in_specs=[pl.BlockSpec(memory_space=pltpu.MemorySpace.SMEM)]
        + [pl.BlockSpec(memory_space=vmem)] * 7,
        out_specs=pl.BlockSpec(memory_space=vmem),
    )(coefs, state, means, lift, embed, kernels, gains, out_weight)


def step_coefficients(sigmas):
    sigma_now = sigmas[:-1]
    sigma_next = sigmas[1:]
    spread = sigma_now * sigma_now + DATA_VAR
    return jnp.stack(
        [
            lax.rsqrt(spread),
            jnp.log(sigma_now) / 4.0,
            DATA_VAR / spread,
            0.5 * sigma_now * lax.rsqrt(spread),
            (sigma_next - sigma_now) / sigma_now,
        ],
        axis=1,
    ).reshape(-1)


def to_lanes(fields, first_lane, lanes):
    batched, variables, pixels = fields.shape
    flat = jnp.transpose(fields, (0, 2, 1)).reshape(batched * pixels, variables)
    return jnp.pad(flat, ((0, 0), (first_lane, lanes - first_lane - variables)))


def make_body(routes):
    def body(
        start_noise,
        reg_means,
        hour_owner,
        member_tile,
        sigmas,
        lift_weight,
        noise_embed,
        section_conv,
        section_gain,
        out_weight,
    ):
        segment_index = lax.axis_index("segment")
        is_first = segment_index == 0
        half_hours = HOURS // lax.axis_size("segment")
        first_hour = segment_index * half_hours
        variables = start_noise.shape[2]
        pixels = start_noise.shape[3]
        channels = section_conv.shape[-1]

        swap = [(0, 1), (1, 0)]
        other_conv = lax.ppermute(section_conv, "segment", swap)
        other_gain = lax.ppermute(section_gain, "segment", swap)
        kernels = jnp.stack(
            [
                jnp.where(is_first, section_conv[0], other_conv[0]),
                jnp.where(is_first, other_conv[0], section_conv[0]),
            ]
        ).reshape(2, 9 * channels, channels)
        gains = jnp.stack(
            [
                jnp.where(is_first, section_gain[0], other_gain[0]),
                jnp.where(is_first, other_gain[0], section_gain[0]),
            ]
        ).astype(jnp.float32)

        owners = lax.dynamic_slice_in_dim(hour_owner, first_hour, half_hours, 0)
        mine = lax.dynamic_slice_in_dim(reg_means[0], first_hour, half_hours, 0)
        is_owner = lax.axis_index("member") == owners
        kept = jnp.where(is_owner[:, None, None, None], mine, 0).astype(mine.dtype)
        means = broadcast_mean(kept, member_tile[0], routes)

        noise = lax.dynamic_slice_in_dim(start_noise[0], first_hour, half_hours, 0)
        states = sigmas[0] * noise
        lift = jnp.pad(lift_weight, ((0, channels - 2 * variables), (0, 0)))
        out_pad = jnp.pad(out_weight, ((0, 0), (0, channels - variables)))
        finished = run_chain(
            step_coefficients(sigmas),
            to_lanes(states, 0, channels),
            to_lanes(means, variables, channels),
            lift,
            noise_embed[None, :],
            kernels,
            gains,
            out_pad,
        )
        finished = finished[:, :variables].reshape(half_hours, pixels, variables)
        return (means + jnp.transpose(finished, (0, 2, 1)))[:, None]

    return body


def solution(mesh):
    placed = (
        P("member", None, None, None),
        P("member", None, None, None, None),
        P(),
        P("member"),
        P(),
        P(),
        P(),
        P("segment", None, None, None),
        P("segment", None),
        P(),
    )
    return jax.shard_map(
        make_body(ring_routes(mesh)),
        mesh=mesh,
        in_specs=placed,
        out_specs=P("segment", "member", None, None),
        check_vma=False,
    )
```

```python
import numpy as np
import jax
import jax.numpy as jnp
from jax import lax
from jax.sharding import PartitionSpec as P
from jax.experimental import pallas as pl
from jax.experimental.pallas import tpu as pltpu

SIDE = 16
HOURS = 4
STEPS = 8


EPSILON = 1e-06
DATA_VAR = 0.25


def ring_routes(mesh):
    devices = np.asarray(mesh.devices)[:, 0]
    coords = [tuple(d.coords[:3]) for d in devices]
    where = {c: i for i, c in enumerate(coords)}
    sizes = [len({c[a] for c in coords}) for a in range(3)]
    axes = [a for a in sorted(range(3), key=lambda a: sizes[a]) if sizes[a] > 1]

    def shift_pairs(axis, distance):
        pairs = []
        for i, c in enumerate(coords):
            moved = list(c)
            moved[axis] = (c[axis] + distance) % sizes[axis]
            pairs.append((i, where[tuple(moved)]))
        return tuple(pairs)

    rings = []
    for axis in axes:
        n = sizes[axis]
        shifts = {d: shift_pairs(axis, d) for d in range(-n + 1, n) if d}
        position = tuple(c[axis] for c in coords)
        rings.append((n, shifts, position))
    return rings


def window_stages(n):
    if n & (n - 1):
        raise ValueError("ring size")
    if n == 2:
        return [(1,)]
    stages = [(1, -1, 2)]
    distance = 4
    while distance < n:
        stages.append((distance,))
        distance *= 2
    return stages


def broadcast_sum(block, rings):
    for n, shifts, _ in rings:
        for stage in window_stages(n):
            arrived = [lax.ppermute(block, "member", shifts[d]) for d in stage]
            for part in arrived:
                block = block + part
    return block


def reversed_pairs(pairs):
    return tuple((j, i) for i, j in pairs)


def broadcast_mean(kept, tile, rings):
    size_z, shifts_z, _ = rings[-1]
    if size_z < 4 or size_z % 2:
        block = broadcast_sum(kept, rings)
        return lax.dynamic_index_in_dim(block, tile, 1, keepdims=False)
    far = range(2, size_z, 2)
    wanted = {
        d: lax.ppermute(tile[None], "member", reversed_pairs(shifts_z[d]))[0] for d in far
    }
    block = broadcast_sum(kept, rings[:-1])
    block = block + lax.ppermute(block, "member", shifts_z[1])
    arrived = [
        lax.ppermute(
            lax.dynamic_index_in_dim(block, wanted[d], 1, keepdims=False), "member", shifts_z[d]
        )
        for d in far
    ]
    mean = lax.dynamic_index_in_dim(block, tile, 1, keepdims=False)
    for part in arrived:
        mean = mean + part
    return mean


def rms_scale(values):
    return values * lax.rsqrt(jnp.mean(values * values, axis=-1, keepdims=True) + EPSILON)


def silu(values):
    return values / (1.0 + jnp.exp(-values))


def chain_kernel(coef_ref, state_ref, means_ref, lift_ref, embed_ref, conv_ref, gain_ref, out_ref, result_ref):
    rows, lanes = state_ref.shape
    pixel = lax.broadcasted_iota(jnp.int32, (rows, lanes), 0) % (SIDE * SIDE)
    col = pixel % SIDE
    col_ok = {b: (col + b >= 0) & (col + b < SIDE) for b in (-1, 1)}
    tiles = rows // (SIDE * SIDE)
    zero_row = jnp.zeros((SIDE, lanes), jnp.bfloat16)

    def shift_rows(moved, a):
        parts = []
        for t in range(tiles):
            tile = moved[t * SIDE * SIDE : (t + 1) * SIDE * SIDE]
            if a == 1:
                parts += [tile[SIDE:], zero_row]
            else:
                parts += [zero_row, tile[:-SIDE]]
        return jnp.concatenate(parts, axis=0)

    def conv(gated, index):
        columns = {}
        for b in (-1, 0, 1):
            moved = gated
            if b:
                moved = jnp.where(col_ok[b], pltpu.roll(gated, (-b) % rows, 0), 0.0)
            columns[b] = moved.astype(jnp.bfloat16)
        windows = []
        for a in (-1, 0, 1):
            for b in (-1, 0, 1):
                windows.append(columns[b] if a == 0 else shift_rows(columns[b], a))
        stacked = jnp.concatenate(windows, axis=1)
        return jnp.dot(stacked, conv_ref[index], preferred_element_type=jnp.float32)

    means = means_ref[...]
    embed = embed_ref[...]
    gain_enc = gain_ref[0:1, :]
    gain_dec = gain_ref[1:2, :]

    def one_step(step, state):
        scale_in = coef_ref[step * 5 + 0]
        level = coef_ref[step * 5 + 1]
        keep_state = coef_ref[step * 5 + 2]
        keep_net = coef_ref[step * 5 + 3]
        move = coef_ref[step * 5 + 4]
        inputs = state * scale_in + means
        lifted = jnp.dot(
            inputs, lift_ref[...], precision=lax.Precision.HIGHEST, preferred_element_type=jnp.float32
        )
        lifted = lifted + level * embed
        gated = silu(rms_scale(lifted) * gain_enc)
        encoded = (lifted + conv(gated, 0)).astype(jnp.bfloat16).astype(jnp.float32)
        gated = silu(rms_scale(encoded) * gain_dec)
        skipped = lifted.astype(jnp.bfloat16).astype(jnp.float32)
        merged = encoded + conv(gated, 1) + skipped
        net_out = jnp.dot(
            silu(rms_scale(merged)),
            out_ref[...],
            precision=lax.Precision.HIGHEST,
            preferred_element_type=jnp.float32,
        )
        denoised = keep_state * state + keep_net * net_out
        return state + move * (state - denoised)

    result_ref[...] = lax.fori_loop(0, STEPS, one_step, state_ref[...], unroll=True)


def run_chain(coefs, state, means, lift, embed, kernels, gains, out_weight):
    vmem = pltpu.MemorySpace.VMEM
    return pl.pallas_call(
        chain_kernel,
        out_shape=jax.ShapeDtypeStruct(state.shape, jnp.float32),
        in_specs=[pl.BlockSpec(memory_space=pltpu.MemorySpace.SMEM)]
        + [pl.BlockSpec(memory_space=vmem)] * 7,
        out_specs=pl.BlockSpec(memory_space=vmem),
    )(coefs, state, means, lift, embed, kernels, gains, out_weight)


def step_coefficients(sigmas):
    sigma_now = sigmas[:-1]
    sigma_next = sigmas[1:]
    spread = sigma_now * sigma_now + DATA_VAR
    return jnp.stack(
        [
            lax.rsqrt(spread),
            jnp.log(sigma_now) / 4.0,
            DATA_VAR / spread,
            0.5 * sigma_now * lax.rsqrt(spread),
            (sigma_next - sigma_now) / sigma_now,
        ],
        axis=1,
    ).reshape(-1)


def to_lanes(fields, first_lane, lanes):
    batched, variables, pixels = fields.shape
    flat = jnp.transpose(fields, (0, 2, 1)).reshape(batched * pixels, variables)
    return jnp.pad(flat, ((0, 0), (first_lane, lanes - first_lane - variables)))


def make_body(routes):
    def body(
        start_noise,
        reg_means,
        hour_owner,
        member_tile,
        sigmas,
        lift_weight,
        noise_embed,
        section_conv,
        section_gain,
        out_weight,
    ):
        segment_index = lax.axis_index("segment")
        is_first = segment_index == 0
        half_hours = HOURS // lax.axis_size("segment")
        first_hour = segment_index * half_hours
        variables = start_noise.shape[2]
        pixels = start_noise.shape[3]
        channels = section_conv.shape[-1]

        swap = [(0, 1), (1, 0)]
        other_conv = lax.ppermute(section_conv, "segment", swap)
        other_gain = lax.ppermute(section_gain, "segment", swap)
        kernels = jnp.stack(
            [
                jnp.where(is_first, section_conv[0], other_conv[0]),
                jnp.where(is_first, other_conv[0], section_conv[0]),
            ]
        ).reshape(2, 9 * channels, channels)
        gains = jnp.stack(
            [
                jnp.where(is_first, section_gain[0], other_gain[0]),
                jnp.where(is_first, other_gain[0], section_gain[0]),
            ]
        ).astype(jnp.float32)

        owners = lax.dynamic_slice_in_dim(hour_owner, first_hour, half_hours, 0)
        mine = lax.dynamic_slice_in_dim(reg_means[0], first_hour, half_hours, 0)
        is_owner = lax.axis_index("member") == owners
        kept = jnp.where(is_owner[:, None, None, None], mine, 0).astype(mine.dtype)
        means = broadcast_mean(kept, member_tile[0], routes)

        noise = lax.dynamic_slice_in_dim(start_noise[0], first_hour, half_hours, 0)
        states = sigmas[0] * noise
        lift = jnp.pad(lift_weight, ((0, channels - 2 * variables), (0, 0)))
        out_pad = jnp.pad(out_weight, ((0, 0), (0, channels - variables)))
        finished = run_chain(
            step_coefficients(sigmas),
            to_lanes(states, 0, channels),
            to_lanes(means, variables, channels),
            lift,
            noise_embed[None, :],
            kernels,
            gains,
            out_pad,
        )
        finished = finished[:, :variables].reshape(half_hours, pixels, variables)
        return (means + jnp.transpose(finished, (0, 2, 1)))[:, None]

    return body


def solution(mesh):
    placed = (
        P("member", None, None, None),
        P("member", None, None, None, None),
        P(),
        P("member"),
        P(),
        P(),
        P(),
        P("segment", None, None, None),
        P("segment", None),
        P(),
    )
    return jax.shard_map(
        make_body(ring_routes(mesh)),
        mesh=mesh,
        in_specs=placed,
        out_specs=P("segment", "member", None, None),
        check_vma=False,
    )
```

```python
import functools

import numpy as np
import jax
import jax.numpy as jnp
from jax import lax
from jax.sharding import PartitionSpec as P
from jax.experimental import pallas as pl
from jax.experimental.pallas import tpu as pltpu

SIDE = 16
HOURS = 4
STEPS = 8


EPSILON = 1e-06
DATA_VAR = 0.25


def ring_routes(mesh):
    devices = np.asarray(mesh.devices)[:, 0]
    coords = [tuple(d.coords[:3]) for d in devices]
    where = {c: i for i, c in enumerate(coords)}
    sizes = [len({c[a] for c in coords}) for a in range(3)]
    axes = [a for a in sorted(range(3), key=lambda a: sizes[a]) if sizes[a] > 1]

    def shift_pairs(axis, distance):
        pairs = []
        for i, c in enumerate(coords):
            moved = list(c)
            moved[axis] = (c[axis] + distance) % sizes[axis]
            pairs.append((i, where[tuple(moved)]))
        return tuple(pairs)

    rings = []
    for axis in axes:
        n = sizes[axis]
        shifts = {d: shift_pairs(axis, d) for d in range(-n + 1, n) if d}
        position = tuple(c[axis] for c in coords)
        rings.append((n, shifts, position))
    return rings


def window_stages(n):
    if n & (n - 1):
        raise ValueError("ring size")
    if n == 2:
        return [(1,)]
    stages = [(1, -1, 2)]
    distance = 4
    while distance < n:
        stages.append((distance,))
        distance *= 2
    return stages


def broadcast_sum(block, rings):
    for n, shifts, _ in rings:
        for stage in window_stages(n):
            arrived = [lax.ppermute(block, "member", shifts[d]) for d in stage]
            for part in arrived:
                block = block + part
    return block


def reversed_pairs(pairs):
    return tuple((j, i) for i, j in pairs)


def broadcast_mean(kept, tile, rings):
    size_z, shifts_z, _ = rings[-1]
    if size_z < 4 or size_z % 2:
        block = broadcast_sum(kept, rings)
        return lax.dynamic_index_in_dim(block, tile, 1, keepdims=False)
    far = range(2, size_z, 2)
    wanted = {
        d: lax.ppermute(tile[None], "member", reversed_pairs(shifts_z[d]))[0] for d in far
    }
    block = broadcast_sum(kept, rings[:-1])
    block = block + lax.ppermute(block, "member", shifts_z[1])
    arrived = [
        lax.ppermute(
            lax.dynamic_index_in_dim(block, wanted[d], 1, keepdims=False), "member", shifts_z[d]
        )
        for d in far
    ]
    mean = lax.dynamic_index_in_dim(block, tile, 1, keepdims=False)
    for part in arrived:
        mean = mean + part
    return mean


def rms_scale(values):
    return values * lax.rsqrt(jnp.mean(values * values, axis=-1, keepdims=True) + EPSILON)


def silu(values):
    return values / (1.0 + jnp.exp(-values))


def chain_kernel(
    variables, coef_ref, state_ref, means_ref, lift_ref, embed_ref, conv_ref, gain_ref, out_ref, result_ref
):
    rows, lanes = state_ref.shape
    pixel = lax.broadcasted_iota(jnp.int32, (rows, lanes), 0) % (SIDE * SIDE)
    col = pixel % SIDE
    col_ok = {b: (col + b >= 0) & (col + b < SIDE) for b in (-1, 1)}
    tiles = rows // (SIDE * SIDE)
    zero_row = jnp.zeros((SIDE, lanes), jnp.bfloat16)

    def shift_rows(moved, a):
        parts = []
        for t in range(tiles):
            tile = moved[t * SIDE * SIDE : (t + 1) * SIDE * SIDE]
            if a == 1:
                parts += [tile[SIDE:], zero_row]
            else:
                parts += [zero_row, tile[:-SIDE]]
        return jnp.concatenate(parts, axis=0)

    def conv(gated, index):
        columns = {}
        for b in (-1, 0, 1):
            moved = gated
            if b:
                moved = jnp.where(col_ok[b], pltpu.roll(gated, (-b) % rows, 0), 0.0)
            columns[b] = moved.astype(jnp.bfloat16)
        windows = []
        for a in (-1, 0, 1):
            for b in (-1, 0, 1):
                windows.append(columns[b] if a == 0 else shift_rows(columns[b], a))
        stacked = jnp.concatenate(windows, axis=1)
        return jnp.dot(stacked, conv_ref[index], preferred_element_type=jnp.float32)

    means = means_ref[...]
    embed = embed_ref[...]
    gain_enc = gain_ref[0:1, :]
    gain_dec = gain_ref[1:2, :]

    def one_step(step, state):
        scale_in = coef_ref[step * 5 + 0]
        level = coef_ref[step * 5 + 1]
        keep_state = coef_ref[step * 5 + 2]
        keep_net = coef_ref[step * 5 + 3]
        move = coef_ref[step * 5 + 4]
        inputs = state * scale_in + means
        lifted = jnp.dot(
            inputs, lift_ref[...], precision=lax.Precision.HIGHEST, preferred_element_type=jnp.float32
        )
        lifted = lifted + level * embed
        gated = silu(rms_scale(lifted) * gain_enc)
        encoded = (lifted + conv(gated, 0)).astype(jnp.bfloat16).astype(jnp.float32)
        gated = silu(rms_scale(encoded) * gain_dec)
        skipped = lifted.astype(jnp.bfloat16).astype(jnp.float32)
        merged = encoded + conv(gated, 1) + skipped
        net_out = jnp.dot(
            silu(rms_scale(merged)),
            out_ref[...],
            precision=lax.Precision.HIGHEST,
            preferred_element_type=jnp.float32,
        )
        denoised = keep_state * state + keep_net * net_out
        return state + move * (state - denoised)

    finished = lax.fori_loop(0, STEPS, one_step, state_ref[...], unroll=True)
    result_ref[...] = finished + pltpu.roll(means, lanes - variables, 1)


def run_chain(variables, coefs, state, means, lift, embed, kernels, gains, out_weight):
    vmem = pltpu.MemorySpace.VMEM
    return pl.pallas_call(
        functools.partial(chain_kernel, variables),
        out_shape=jax.ShapeDtypeStruct(state.shape, jnp.float32),
        in_specs=[pl.BlockSpec(memory_space=pltpu.MemorySpace.SMEM)]
        + [pl.BlockSpec(memory_space=vmem)] * 7,
        out_specs=pl.BlockSpec(memory_space=vmem),
    )(coefs, state, means, lift, embed, kernels, gains, out_weight)


def step_coefficients(sigmas):
    sigma_now = sigmas[:-1]
    sigma_next = sigmas[1:]
    spread = sigma_now * sigma_now + DATA_VAR
    return jnp.stack(
        [
            lax.rsqrt(spread),
            jnp.log(sigma_now) / 4.0,
            DATA_VAR / spread,
            0.5 * sigma_now * lax.rsqrt(spread),
            (sigma_next - sigma_now) / sigma_now,
        ],
        axis=1,
    ).reshape(-1)


def to_lanes(fields, first_lane, lanes):
    batched, variables, pixels = fields.shape
    flat = jnp.transpose(fields, (0, 2, 1)).reshape(batched * pixels, variables)
    return jnp.pad(flat, ((0, 0), (first_lane, lanes - first_lane - variables)))


def make_body(routes):
    def body(
        start_noise,
        reg_means,
        hour_owner,
        member_tile,
        sigmas,
        lift_weight,
        noise_embed,
        section_conv,
        section_gain,
        out_weight,
    ):
        segment_index = lax.axis_index("segment")
        is_first = segment_index == 0
        half_hours = HOURS // lax.axis_size("segment")
        first_hour = segment_index * half_hours
        variables = start_noise.shape[2]
        pixels = start_noise.shape[3]
        channels = section_conv.shape[-1]

        swap = [(0, 1), (1, 0)]
        other_conv = lax.ppermute(section_conv, "segment", swap)
        other_gain = lax.ppermute(section_gain, "segment", swap)
        kernels = jnp.stack(
            [
                jnp.where(is_first, section_conv[0], other_conv[0]),
                jnp.where(is_first, other_conv[0], section_conv[0]),
            ]
        ).reshape(2, 9 * channels, channels)
        gains = jnp.stack(
            [
                jnp.where(is_first, section_gain[0], other_gain[0]),
                jnp.where(is_first, other_gain[0], section_gain[0]),
            ]
        ).astype(jnp.float32)

        owners = lax.dynamic_slice_in_dim(hour_owner, first_hour, half_hours, 0)
        mine = lax.dynamic_slice_in_dim(reg_means[0], first_hour, half_hours, 0)
        is_owner = lax.axis_index("member") == owners
        kept = jnp.where(is_owner[:, None, None, None], mine, 0).astype(mine.dtype)
        means = broadcast_mean(kept, member_tile[0], routes)

        noise = lax.dynamic_slice_in_dim(start_noise[0], first_hour, half_hours, 0)
        states = sigmas[0] * noise
        lift = jnp.pad(lift_weight, ((0, channels - 2 * variables), (0, 0)))
        out_pad = jnp.pad(out_weight, ((0, 0), (0, channels - variables)))
        finished = run_chain(
            variables,
            step_coefficients(sigmas),
            to_lanes(states, 0, channels),
            to_lanes(means, variables, channels),
            lift,
            noise_embed[None, :],
            kernels,
            gains,
            out_pad,
        )
        finished = finished[:, :variables].reshape(half_hours, pixels, variables)
        return jnp.transpose(finished, (0, 2, 1))[:, None]

    return body


def solution(mesh):
    placed = (
        P("member", None, None, None),
        P("member", None, None, None, None),
        P(),
        P("member"),
        P(),
        P(),
        P(),
        P("segment", None, None, None),
        P("segment", None),
        P(),
    )
    return jax.shard_map(
        make_body(ring_routes(mesh)),
        mesh=mesh,
        in_specs=placed,
        out_specs=P("segment", "member", None, None),
        check_vma=False,
    )
```

```python
import numpy as np
import jax
import jax.numpy as jnp
from jax import lax
from jax.sharding import PartitionSpec as P
from jax.experimental import pallas as pl
from jax.experimental.pallas import tpu as pltpu

SIDE = 16
HOURS = 4
STEPS = 8


EPSILON = 1e-06
DATA_VAR = 0.25


def ring_routes(mesh):
    devices = np.asarray(mesh.devices)[:, 0]
    coords = [tuple(d.coords[:3]) for d in devices]
    where = {c: i for i, c in enumerate(coords)}
    sizes = [len({c[a] for c in coords}) for a in range(3)]
    axes = [a for a in sorted(range(3), key=lambda a: sizes[a]) if sizes[a] > 1]

    def shift_pairs(axis, distance):
        pairs = []
        for i, c in enumerate(coords):
            moved = list(c)
            moved[axis] = (c[axis] + distance) % sizes[axis]
            pairs.append((i, where[tuple(moved)]))
        return tuple(pairs)

    rings = []
    for axis in axes:
        n = sizes[axis]
        shifts = {d: shift_pairs(axis, d) for d in range(-n + 1, n) if d}
        position = tuple(c[axis] for c in coords)
        rings.append((n, shifts, position))
    return rings


def window_stages(n):
    if n & (n - 1):
        raise ValueError("ring size")
    if n == 2:
        return [(1,)]
    stages = [(1, -1, 2)]
    distance = 4
    while distance < n:
        stages.append((distance,))
        distance *= 2
    return stages


def broadcast_sum(block, rings):
    for n, shifts, _ in rings:
        for stage in window_stages(n):
            arrived = [lax.ppermute(block, "member", shifts[d]) for d in stage]
            for part in arrived:
                block = block + part
    return block


def reversed_pairs(pairs):
    return tuple((j, i) for i, j in pairs)


def broadcast_mean(kept, tile, rings):
    size_z, shifts_z, _ = rings[-1]
    if size_z < 4 or size_z % 2:
        block = broadcast_sum(kept, rings)
        return lax.dynamic_index_in_dim(block, tile, 1, keepdims=False)
    known = {
        d: lax.ppermute(tile[None], "member", reversed_pairs(shifts_z[d]))[0]
        for d in range(1, size_z)
    }
    known[0] = tile
    evens = range(0, size_z, 2)
    block = broadcast_sum(kept, rings[:-1])
    sent = jnp.take(block, jnp.stack([known[1 + e] for e in evens]), axis=1, mode="clip")
    block = jnp.take(block, jnp.stack([known[e] for e in evens]), axis=1, mode="clip")
    block = block + lax.ppermute(sent, "member", shifts_z[1])
    arrived = [
        lax.ppermute(block[:, slot], "member", shifts_z[e]) for slot, e in enumerate(evens) if e
    ]
    mean = block[:, 0]
    for part in arrived:
        mean = mean + part
    return mean


def rms_scale(values):
    return values * lax.rsqrt(jnp.mean(values * values, axis=-1, keepdims=True) + EPSILON)


def silu(values):
    return values / (1.0 + jnp.exp(-values))


def chain_kernel(coef_ref, state_ref, means_ref, lift_ref, embed_ref, conv_ref, gain_ref, out_ref, result_ref):
    rows, lanes = state_ref.shape
    pixel = lax.broadcasted_iota(jnp.int32, (rows, lanes), 0) % (SIDE * SIDE)
    col = pixel % SIDE
    col_ok = {b: (col + b >= 0) & (col + b < SIDE) for b in (-1, 1)}
    tiles = rows // (SIDE * SIDE)
    zero_row = jnp.zeros((SIDE, lanes), jnp.bfloat16)

    def shift_rows(moved, a):
        parts = []
        for t in range(tiles):
            tile = moved[t * SIDE * SIDE : (t + 1) * SIDE * SIDE]
            if a == 1:
                parts += [tile[SIDE:], zero_row]
            else:
                parts += [zero_row, tile[:-SIDE]]
        return jnp.concatenate(parts, axis=0)

    def conv(gated, index):
        columns = {}
        for b in (-1, 0, 1):
            moved = gated
            if b:
                moved = jnp.where(col_ok[b], pltpu.roll(gated, (-b) % rows, 0), 0.0)
            columns[b] = moved.astype(jnp.bfloat16)
        windows = []
        for a in (-1, 0, 1):
            for b in (-1, 0, 1):
                windows.append(columns[b] if a == 0 else shift_rows(columns[b], a))
        stacked = jnp.concatenate(windows, axis=1)
        return jnp.dot(stacked, conv_ref[index], preferred_element_type=jnp.float32)

    means = means_ref[...]
    embed = embed_ref[...]
    gain_enc = gain_ref[0:1, :]
    gain_dec = gain_ref[1:2, :]

    def one_step(step, state):
        scale_in = coef_ref[step * 5 + 0]
        level = coef_ref[step * 5 + 1]
        keep_state = coef_ref[step * 5 + 2]
        keep_net = coef_ref[step * 5 + 3]
        move = coef_ref[step * 5 + 4]
        inputs = state * scale_in + means
        lifted = jnp.dot(
            inputs, lift_ref[...], precision=lax.Precision.HIGHEST, preferred_element_type=jnp.float32
        )
        lifted = lifted + level * embed
        gated = silu(rms_scale(lifted) * gain_enc)
        encoded = (lifted + conv(gated, 0)).astype(jnp.bfloat16).astype(jnp.float32)
        gated = silu(rms_scale(encoded) * gain_dec)
        skipped = lifted.astype(jnp.bfloat16).astype(jnp.float32)
        merged = encoded + conv(gated, 1) + skipped
        net_out = jnp.dot(
            silu(rms_scale(merged)),
            out_ref[...],
            precision=lax.Precision.HIGHEST,
            preferred_element_type=jnp.float32,
        )
        denoised = keep_state * state + keep_net * net_out
        return state + move * (state - denoised)

    result_ref[...] = lax.fori_loop(0, STEPS, one_step, state_ref[...], unroll=True)


def run_chain(coefs, state, means, lift, embed, kernels, gains, out_weight):
    vmem = pltpu.MemorySpace.VMEM
    return pl.pallas_call(
        chain_kernel,
        out_shape=jax.ShapeDtypeStruct(state.shape, jnp.float32),
        in_specs=[pl.BlockSpec(memory_space=pltpu.MemorySpace.SMEM)]
        + [pl.BlockSpec(memory_space=vmem)] * 7,
        out_specs=pl.BlockSpec(memory_space=vmem),
    )(coefs, state, means, lift, embed, kernels, gains, out_weight)


def step_coefficients(sigmas):
    sigma_now = sigmas[:-1]
    sigma_next = sigmas[1:]
    spread = sigma_now * sigma_now + DATA_VAR
    return jnp.stack(
        [
            lax.rsqrt(spread),
            jnp.log(sigma_now) / 4.0,
            DATA_VAR / spread,
            0.5 * sigma_now * lax.rsqrt(spread),
            (sigma_next - sigma_now) / sigma_now,
        ],
        axis=1,
    ).reshape(-1)


def to_lanes(fields, first_lane, lanes):
    batched, variables, pixels = fields.shape
    flat = jnp.transpose(fields, (0, 2, 1)).reshape(batched * pixels, variables)
    return jnp.pad(flat, ((0, 0), (first_lane, lanes - first_lane - variables)))


def make_body(routes):
    def body(
        start_noise,
        reg_means,
        hour_owner,
        member_tile,
        sigmas,
        lift_weight,
        noise_embed,
        section_conv,
        section_gain,
        out_weight,
    ):
        segment_index = lax.axis_index("segment")
        is_first = segment_index == 0
        half_hours = HOURS // lax.axis_size("segment")
        first_hour = segment_index * half_hours
        variables = start_noise.shape[2]
        pixels = start_noise.shape[3]
        channels = section_conv.shape[-1]

        swap = [(0, 1), (1, 0)]
        other_conv = lax.ppermute(section_conv, "segment", swap)
        other_gain = lax.ppermute(section_gain, "segment", swap)
        kernels = jnp.stack(
            [
                jnp.where(is_first, section_conv[0], other_conv[0]),
                jnp.where(is_first, other_conv[0], section_conv[0]),
            ]
        ).reshape(2, 9 * channels, channels)
        gains = jnp.stack(
            [
                jnp.where(is_first, section_gain[0], other_gain[0]),
                jnp.where(is_first, other_gain[0], section_gain[0]),
            ]
        ).astype(jnp.float32)

        owners = lax.dynamic_slice_in_dim(hour_owner, first_hour, half_hours, 0)
        mine = lax.dynamic_slice_in_dim(reg_means[0], first_hour, half_hours, 0)
        is_owner = lax.axis_index("member") == owners
        kept = jnp.where(is_owner[:, None, None, None], mine, 0).astype(mine.dtype)
        means = broadcast_mean(kept, member_tile[0], routes)

        noise = lax.dynamic_slice_in_dim(start_noise[0], first_hour, half_hours, 0)
        states = sigmas[0] * noise
        lift = jnp.pad(lift_weight, ((0, channels - 2 * variables), (0, 0)))
        out_pad = jnp.pad(out_weight, ((0, 0), (0, channels - variables)))
        finished = run_chain(
            step_coefficients(sigmas),
            to_lanes(states, 0, channels),
            to_lanes(means, variables, channels),
            lift,
            noise_embed[None, :],
            kernels,
            gains,
            out_pad,
        )
        finished = finished[:, :variables].reshape(half_hours, pixels, variables)
        return (means + jnp.transpose(finished, (0, 2, 1)))[:, None]

    return body


def solution(mesh):
    placed = (
        P("member", None, None, None),
        P("member", None, None, None, None),
        P(),
        P("member"),
        P(),
        P(),
        P(),
        P("segment", None, None, None),
        P("segment", None),
        P(),
    )
    return jax.shard_map(
        make_body(ring_routes(mesh)),
        mesh=mesh,
        in_specs=placed,
        out_specs=P("segment", "member", None, None),
        check_vma=False,
    )
```

```python
import numpy as np
import jax
import jax.numpy as jnp
from jax import lax
from jax.sharding import PartitionSpec as P
from jax.experimental import pallas as pl
from jax.experimental.pallas import tpu as pltpu

SIDE = 16
HOURS = 4
STEPS = 8


EPSILON = 1e-06
DATA_VAR = 0.25


def ring_routes(mesh):
    devices = np.asarray(mesh.devices)[:, 0]
    coords = [tuple(d.coords[:3]) for d in devices]
    where = {c: i for i, c in enumerate(coords)}
    sizes = [len({c[a] for c in coords}) for a in range(3)]
    axes = [a for a in sorted(range(3), key=lambda a: sizes[a]) if sizes[a] > 1]

    def shift_pairs(axis, distance):
        pairs = []
        for i, c in enumerate(coords):
            moved = list(c)
            moved[axis] = (c[axis] + distance) % sizes[axis]
            pairs.append((i, where[tuple(moved)]))
        return tuple(pairs)

    rings = []
    for axis in axes:
        n = sizes[axis]
        shifts = {d: shift_pairs(axis, d) for d in range(-n + 1, n) if d}
        position = tuple(c[axis] for c in coords)
        rings.append((n, shifts, position))
    return rings


def window_stages(n):
    if n & (n - 1):
        raise ValueError("ring size")
    if n == 2:
        return [(1,)]
    stages = [(1, -1, 2)]
    distance = 4
    while distance < n:
        stages.append((distance,))
        distance *= 2
    return stages


def broadcast_sum(block, rings):
    for n, shifts, _ in rings:
        for stage in window_stages(n):
            arrived = [lax.ppermute(block, "member", shifts[d]) for d in stage]
            for part in arrived:
                block = block + part
    return block


def reversed_pairs(pairs):
    return tuple((j, i) for i, j in pairs)


def broadcast_mean(kept, tile, rings):
    size_z, shifts_z, _ = rings[-1]
    if size_z < 4 or size_z % 2:
        block = broadcast_sum(kept, rings)
        return lax.dynamic_index_in_dim(block, tile, 1, keepdims=False)
    block = broadcast_sum(kept, rings[:1])
    later, block = lax.optimization_barrier((tile, block))
    known = {
        d: lax.ppermute(later[None], "member", reversed_pairs(shifts_z[d]))[0]
        for d in range(1, size_z)
    }
    known[0] = tile
    evens = range(0, size_z, 2)
    block = broadcast_sum(block, rings[1:-1])
    sent = jnp.take(block, jnp.stack([known[1 + e] for e in evens]), axis=1, mode="clip")
    block = jnp.take(block, jnp.stack([known[e] for e in evens]), axis=1, mode="clip")
    block = block + lax.ppermute(sent, "member", shifts_z[1])
    arrived = [
        lax.ppermute(block[:, slot], "member", shifts_z[e]) for slot, e in enumerate(evens) if e
    ]
    mean = block[:, 0]
    for part in arrived:
        mean = mean + part
    return mean


def rms_scale(values):
    return values * lax.rsqrt(jnp.mean(values * values, axis=-1, keepdims=True) + EPSILON)


def silu(values):
    return values / (1.0 + jnp.exp(-values))


def chain_kernel(coef_ref, state_ref, means_ref, lift_ref, embed_ref, conv_ref, gain_ref, out_ref, result_ref):
    rows, lanes = state_ref.shape
    pixel = lax.broadcasted_iota(jnp.int32, (rows, lanes), 0) % (SIDE * SIDE)
    col = pixel % SIDE
    col_ok = {b: (col + b >= 0) & (col + b < SIDE) for b in (-1, 1)}
    tiles = rows // (SIDE * SIDE)
    zero_row = jnp.zeros((SIDE, lanes), jnp.bfloat16)

    def shift_rows(moved, a):
        parts = []
        for t in range(tiles):
            tile = moved[t * SIDE * SIDE : (t + 1) * SIDE * SIDE]
            if a == 1:
                parts += [tile[SIDE:], zero_row]
            else:
                parts += [zero_row, tile[:-SIDE]]
        return jnp.concatenate(parts, axis=0)

    def conv(gated, index):
        columns = {}
        for b in (-1, 0, 1):
            moved = gated
            if b:
                moved = jnp.where(col_ok[b], pltpu.roll(gated, (-b) % rows, 0), 0.0)
            columns[b] = moved.astype(jnp.bfloat16)
        windows = []
        for a in (-1, 0, 1):
            for b in (-1, 0, 1):
                windows.append(columns[b] if a == 0 else shift_rows(columns[b], a))
        stacked = jnp.concatenate(windows, axis=1)
        return jnp.dot(stacked, conv_ref[index], preferred_element_type=jnp.float32)

    means = means_ref[...]
    embed = embed_ref[...]
    gain_enc = gain_ref[0:1, :]
    gain_dec = gain_ref[1:2, :]

    def one_step(step, state):
        scale_in = coef_ref[step * 5 + 0]
        level = coef_ref[step * 5 + 1]
        keep_state = coef_ref[step * 5 + 2]
        keep_net = coef_ref[step * 5 + 3]
        move = coef_ref[step * 5 + 4]
        inputs = state * scale_in + means
        lifted = jnp.dot(
            inputs, lift_ref[...], precision=lax.Precision.HIGHEST, preferred_element_type=jnp.float32
        )
        lifted = lifted + level * embed
        gated = silu(rms_scale(lifted) * gain_enc)
        encoded = (lifted + conv(gated, 0)).astype(jnp.bfloat16).astype(jnp.float32)
        gated = silu(rms_scale(encoded) * gain_dec)
        skipped = lifted.astype(jnp.bfloat16).astype(jnp.float32)
        merged = encoded + conv(gated, 1) + skipped
        net_out = jnp.dot(
            silu(rms_scale(merged)),
            out_ref[...],
            precision=lax.Precision.HIGHEST,
            preferred_element_type=jnp.float32,
        )
        denoised = keep_state * state + keep_net * net_out
        return state + move * (state - denoised)

    result_ref[...] = lax.fori_loop(0, STEPS, one_step, state_ref[...], unroll=True)


def run_chain(coefs, state, means, lift, embed, kernels, gains, out_weight):
    vmem = pltpu.MemorySpace.VMEM
    return pl.pallas_call(
        chain_kernel,
        out_shape=jax.ShapeDtypeStruct(state.shape, jnp.float32),
        in_specs=[pl.BlockSpec(memory_space=pltpu.MemorySpace.SMEM)]
        + [pl.BlockSpec(memory_space=vmem)] * 7,
        out_specs=pl.BlockSpec(memory_space=vmem),
    )(coefs, state, means, lift, embed, kernels, gains, out_weight)


def step_coefficients(sigmas):
    sigma_now = sigmas[:-1]
    sigma_next = sigmas[1:]
    spread = sigma_now * sigma_now + DATA_VAR
    return jnp.stack(
        [
            lax.rsqrt(spread),
            jnp.log(sigma_now) / 4.0,
            DATA_VAR / spread,
            0.5 * sigma_now * lax.rsqrt(spread),
            (sigma_next - sigma_now) / sigma_now,
        ],
        axis=1,
    ).reshape(-1)


def to_lanes(fields, first_lane, lanes):
    batched, variables, pixels = fields.shape
    flat = jnp.transpose(fields, (0, 2, 1)).reshape(batched * pixels, variables)
    return jnp.pad(flat, ((0, 0), (first_lane, lanes - first_lane - variables)))


def make_body(routes):
    def body(
        start_noise,
        reg_means,
        hour_owner,
        member_tile,
        sigmas,
        lift_weight,
        noise_embed,
        section_conv,
        section_gain,
        out_weight,
    ):
        segment_index = lax.axis_index("segment")
        is_first = segment_index == 0
        half_hours = HOURS // lax.axis_size("segment")
        first_hour = segment_index * half_hours
        variables = start_noise.shape[2]
        pixels = start_noise.shape[3]
        channels = section_conv.shape[-1]

        swap = [(0, 1), (1, 0)]
        other_conv = lax.ppermute(section_conv, "segment", swap)
        other_gain = lax.ppermute(section_gain, "segment", swap)
        kernels = jnp.stack(
            [
                jnp.where(is_first, section_conv[0], other_conv[0]),
                jnp.where(is_first, other_conv[0], section_conv[0]),
            ]
        ).reshape(2, 9 * channels, channels)
        gains = jnp.stack(
            [
                jnp.where(is_first, section_gain[0], other_gain[0]),
                jnp.where(is_first, other_gain[0], section_gain[0]),
            ]
        ).astype(jnp.float32)

        owners = lax.dynamic_slice_in_dim(hour_owner, first_hour, half_hours, 0)
        mine = lax.dynamic_slice_in_dim(reg_means[0], first_hour, half_hours, 0)
        is_owner = lax.axis_index("member") == owners
        kept = jnp.where(is_owner[:, None, None, None], mine, 0).astype(mine.dtype)
        means = broadcast_mean(kept, member_tile[0], routes)

        noise = lax.dynamic_slice_in_dim(start_noise[0], first_hour, half_hours, 0)
        states = sigmas[0] * noise
        lift = jnp.pad(lift_weight, ((0, channels - 2 * variables), (0, 0)))
        out_pad = jnp.pad(out_weight, ((0, 0), (0, channels - variables)))
        finished = run_chain(
            step_coefficients(sigmas),
            to_lanes(states, 0, channels),
            to_lanes(means, variables, channels),
            lift,
            noise_embed[None, :],
            kernels,
            gains,
            out_pad,
        )
        finished = finished[:, :variables].reshape(half_hours, pixels, variables)
        return (means + jnp.transpose(finished, (0, 2, 1)))[:, None]

    return body


def solution(mesh):
    placed = (
        P("member", None, None, None),
        P("member", None, None, None, None),
        P(),
        P("member"),
        P(),
        P(),
        P(),
        P("segment", None, None, None),
        P("segment", None),
        P(),
    )
    return jax.shard_map(
        make_body(ring_routes(mesh)),
        mesh=mesh,
        in_specs=placed,
        out_specs=P("segment", "member", None, None),
        check_vma=False,
    )
```

```python
import numpy as np
import jax
import jax.numpy as jnp
from jax import lax
from jax.sharding import PartitionSpec as P
from jax.experimental import pallas as pl
from jax.experimental.pallas import tpu as pltpu

SIDE = 16
HOURS = 4
STEPS = 8


EPSILON = 1e-06
DATA_VAR = 0.25


def ring_routes(mesh):
    devices = np.asarray(mesh.devices)[:, 0]
    coords = [tuple(d.coords[:3]) for d in devices]
    where = {c: i for i, c in enumerate(coords)}
    sizes = [len({c[a] for c in coords}) for a in range(3)]
    axes = [a for a in sorted(range(3), key=lambda a: sizes[a]) if sizes[a] > 1]

    def shift_pairs(axis, distance):
        pairs = []
        for i, c in enumerate(coords):
            moved = list(c)
            moved[axis] = (c[axis] + distance) % sizes[axis]
            pairs.append((i, where[tuple(moved)]))
        return tuple(pairs)

    rings = []
    for axis in axes:
        n = sizes[axis]
        shifts = {d: shift_pairs(axis, d) for d in range(-n + 1, n) if d}
        position = tuple(c[axis] for c in coords)
        rings.append((n, shifts, position))
    return rings


def window_stages(n):
    if n & (n - 1):
        raise ValueError("ring size")
    if n == 2:
        return [(1,)]
    stages = [(1, -1, 2)]
    distance = 4
    while distance < n:
        stages.append((distance,))
        distance *= 2
    return stages


def broadcast_sum(block, rings):
    for n, shifts, _ in rings:
        for stage in window_stages(n):
            arrived = [lax.ppermute(block, "member", shifts[d]) for d in stage]
            for part in arrived:
                block = block + part
    return block


def reversed_pairs(pairs):
    return tuple((j, i) for i, j in pairs)


def broadcast_mean(kept, tile, rings):
    size_z, shifts_z, _ = rings[-1]
    if size_z < 4 or size_z % 2:
        block = broadcast_sum(kept, rings)
        return lax.dynamic_index_in_dim(block, tile, 1, keepdims=False)
    far = range(2, size_z, 2)
    wanted = {
        d: lax.ppermute(tile[None], "member", reversed_pairs(shifts_z[d]))[0] for d in far
    }
    block = broadcast_sum(kept, rings[:-1])
    block = block + lax.ppermute(block, "member", shifts_z[1])
    arrived = [
        lax.ppermute(
            lax.dynamic_index_in_dim(block, wanted[d], 1, keepdims=False), "member", shifts_z[d]
        )
        for d in far
    ]
    mean = lax.dynamic_index_in_dim(block, tile, 1, keepdims=False)
    for part in arrived:
        mean = mean + part
    return mean


def rms_scale(values):
    return values * lax.rsqrt(jnp.mean(values * values, axis=-1, keepdims=True) + EPSILON)


def silu(values):
    return values / (1.0 + jnp.exp(-values))


def chain_kernel(coef_ref, state_ref, means_ref, lift_ref, embed_ref, conv_ref, gain_ref, out_ref, result_ref):
    rows, lanes = state_ref.shape
    pixel = lax.broadcasted_iota(jnp.int32, (rows, lanes), 0) % (SIDE * SIDE)
    col = pixel % SIDE
    col_ok = {b: (col + b >= 0) & (col + b < SIDE) for b in (-1, 1)}
    tiles = rows // (SIDE * SIDE)
    zero_row = jnp.zeros((SIDE, lanes), jnp.bfloat16)

    def shift_rows(moved, a):
        parts = []
        for t in range(tiles):
            tile = moved[t * SIDE * SIDE : (t + 1) * SIDE * SIDE]
            if a == 1:
                parts += [tile[SIDE:], zero_row]
            else:
                parts += [zero_row, tile[:-SIDE]]
        return jnp.concatenate(parts, axis=0)

    def conv(gated, index):
        columns = {}
        for b in (-1, 0, 1):
            moved = gated
            if b:
                moved = jnp.where(col_ok[b], pltpu.roll(gated, (-b) % rows, 0), 0.0)
            columns[b] = moved.astype(jnp.bfloat16)
        windows = []
        for a in (-1, 0, 1):
            for b in (-1, 0, 1):
                windows.append(columns[b] if a == 0 else shift_rows(columns[b], a))
        stacked = jnp.concatenate(windows, axis=1)
        return jnp.dot(stacked, conv_ref[index], preferred_element_type=jnp.float32)

    means = means_ref[...]
    embed = embed_ref[...]
    gain_enc = gain_ref[0:1, :]
    gain_dec = gain_ref[1:2, :]

    def one_step(step, state):
        scale_in = coef_ref[step * 5 + 0]
        level = coef_ref[step * 5 + 1]
        keep_state = coef_ref[step * 5 + 2]
        keep_net = coef_ref[step * 5 + 3]
        move = coef_ref[step * 5 + 4]
        inputs = state * scale_in + means
        lifted = jnp.dot(
            inputs, lift_ref[...], precision=lax.Precision.HIGHEST, preferred_element_type=jnp.float32
        )
        lifted = lifted + level * embed
        gated = silu(rms_scale(lifted) * gain_enc)
        encoded = (lifted + conv(gated, 0)).astype(jnp.bfloat16).astype(jnp.float32)
        gated = silu(rms_scale(encoded) * gain_dec)
        skipped = lifted.astype(jnp.bfloat16).astype(jnp.float32)
        merged = encoded + conv(gated, 1) + skipped
        net_out = jnp.dot(
            silu(rms_scale(merged)),
            out_ref[...],
            precision=lax.Precision.HIGHEST,
            preferred_element_type=jnp.float32,
        )
        denoised = keep_state * state + keep_net * net_out
        return state + move * (state - denoised)

    result_ref[...] = lax.fori_loop(0, STEPS, one_step, state_ref[...], unroll=True)


def run_chain(coefs, state, means, lift, embed, kernels, gains, out_weight):
    vmem = pltpu.MemorySpace.VMEM
    return pl.pallas_call(
        chain_kernel,
        out_shape=jax.ShapeDtypeStruct(state.shape, jnp.float32),
        in_specs=[pl.BlockSpec(memory_space=pltpu.MemorySpace.SMEM)]
        + [pl.BlockSpec(memory_space=vmem)] * 7,
        out_specs=pl.BlockSpec(memory_space=vmem),
    )(coefs, state, means, lift, embed, kernels, gains, out_weight)


def step_coefficients(sigmas):
    sigma_now = sigmas[:-1]
    sigma_next = sigmas[1:]
    spread = sigma_now * sigma_now + DATA_VAR
    return jnp.stack(
        [
            lax.rsqrt(spread),
            jnp.log(sigma_now) / 4.0,
            DATA_VAR / spread,
            0.5 * sigma_now * lax.rsqrt(spread),
            (sigma_next - sigma_now) / sigma_now,
        ],
        axis=1,
    ).reshape(-1)


def to_lanes(fields, first_lane, lanes):
    batched, variables, pixels = fields.shape
    flat = jnp.transpose(fields, (0, 2, 1)).reshape(batched * pixels, variables)
    return jnp.pad(flat, ((0, 0), (first_lane, lanes - first_lane - variables)))


def make_body(routes):
    def body(
        start_noise,
        reg_means,
        hour_owner,
        member_tile,
        sigmas,
        lift_weight,
        noise_embed,
        section_conv,
        section_gain,
        out_weight,
    ):
        segment_index = lax.axis_index("segment")
        is_first = segment_index == 0
        half_hours = HOURS // lax.axis_size("segment")
        first_hour = segment_index * half_hours
        variables = start_noise.shape[2]
        pixels = start_noise.shape[3]
        channels = section_conv.shape[-1]

        swap = [(0, 1), (1, 0)]
        taps = section_conv.shape[1]
        packed = jnp.concatenate(
            [section_conv.reshape(1, taps * channels, channels), section_gain[:, None, :]], axis=1
        )
        other = lax.ppermute(packed, "segment", swap)
        other_conv = other[:, : taps * channels].reshape(section_conv.shape)
        other_gain = other[:, taps * channels]
        kernels = jnp.stack(
            [
                jnp.where(is_first, section_conv[0], other_conv[0]),
                jnp.where(is_first, other_conv[0], section_conv[0]),
            ]
        ).reshape(2, 9 * channels, channels)
        gains = jnp.stack(
            [
                jnp.where(is_first, section_gain[0], other_gain[0]),
                jnp.where(is_first, other_gain[0], section_gain[0]),
            ]
        ).astype(jnp.float32)

        owners = lax.dynamic_slice_in_dim(hour_owner, first_hour, half_hours, 0)
        mine = lax.dynamic_slice_in_dim(reg_means[0], first_hour, half_hours, 0)
        is_owner = lax.axis_index("member") == owners
        kept = jnp.where(is_owner[:, None, None, None], mine, 0).astype(mine.dtype)
        means = broadcast_mean(kept, member_tile[0], routes)

        noise = lax.dynamic_slice_in_dim(start_noise[0], first_hour, half_hours, 0)
        states = sigmas[0] * noise
        lift = jnp.pad(lift_weight, ((0, channels - 2 * variables), (0, 0)))
        out_pad = jnp.pad(out_weight, ((0, 0), (0, channels - variables)))
        finished = run_chain(
            step_coefficients(sigmas),
            to_lanes(states, 0, channels),
            to_lanes(means, variables, channels),
            lift,
            noise_embed[None, :],
            kernels,
            gains,
            out_pad,
        )
        finished = finished[:, :variables].reshape(half_hours, pixels, variables)
        return (means + jnp.transpose(finished, (0, 2, 1)))[:, None]

    return body


def solution(mesh):
    placed = (
        P("member", None, None, None),
        P("member", None, None, None, None),
        P(),
        P("member"),
        P(),
        P(),
        P(),
        P("segment", None, None, None),
        P("segment", None),
        P(),
    )
    return jax.shard_map(
        make_body(ring_routes(mesh)),
        mesh=mesh,
        in_specs=placed,
        out_specs=P("segment", "member", None, None),
        check_vma=False,
    )
```
